256 devices in a mesh: tile: 16 (over z, x_lo), obj: 16 (over x_hi, y, core).
Axes of the slice: x: 4 (x_hi: 2, x_lo: 2; x = x_hi * 2 + x_lo), y: 4, z: 8, core: 2. Of those that a mesh axis runs over, the one named last changes fastest.
Arguments:
- adjoint_in: float32 [256, 2, 256, 1024], P('obj', None, 'tile'), may hold values from -6 to 6
- checkpoint_store: float32 [64, 2, 256, 1024], P('obj', None, 'tile'), may hold values from 1900 to 2500, as said below
- interval: int32 [1], replicated, may hold values from 0 to 63
- sea_mask: int32 [256, 1024], P('tile'), may hold values 0 or 1
- zonal_speed: float32 [256, 1024], P('tile'), may hold values from -0.45 to 0.45
- mixing: float32 [256, 1024], P('tile'), may hold values from 0.02 to 0.2
- piston: float32 [256, 32], P('tile'), may hold values from 0.1 to 0.9
- cell_area: float32 [256, 32], P('tile'), may hold values from 5 to 50
- region: int32 [256, 32], P('tile'), may hold values from 0 to 255
Outputs:
- adjoint_out: float32 [256, 2, 256, 1024], P('obj', None, 'tile')
The draws below stay inside these ranges and needn't reach their ends.
Inputs may be any that keep to these rules, and one draw needn't show every extreme that they name: region numbers name objectives. `checkpoint_store`: dissolved carbon lies in 1900 to 2100 and alkalinity exceeds it by 200 to 400 in every cell.
All inputs are finite; a program needn't handle non-finite values. No bound on the sum of `sea_mask` on one device may be relied on, other than what follows from the above.
Results may differ from the reference program's by a relative error of at most 0.0003.
Values sent between devices are 32-bit elements; how exact they have to be, the bound alone decides.
No kernel may reach another device: no remote copies, remote signals or barrier semaphores. Data moves between devices by JAX's collectives and lax.ppermute only.
A program may use at most 64 MiB of HBM per device.

```python
import math
import jax
import jax.numpy as jnp
from jax import lax

ROWS = 32
LEVELS = 32
SLOT_DEV = 4
NEWTON = 4
CELLS = 1024
NI = 256
OBJ = 256
SLOTS = 64
N_OBJ = 16


def draw_checkpoint_store(key, part):
    first_key, second_key = jax.random.split(jax.random.fold_in(key, 11))
    shape = (SLOTS, 1, NI, LEVELS * ROWS)
    carbon = 2000.0 + 30.0 * jnp.clip(jax.random.normal(first_key, shape, jnp.float32), -3.0, 3.0)
    excess = 300.0 + 30.0 * jnp.clip(jax.random.normal(second_key, shape, jnp.float32), -3.0, 3.0)
    return jnp.concatenate([carbon, carbon + excess], axis=1).astype(jnp.float32)


def set_ends(drawn, rng, least, largest):
    place = [jax.random.randint(jax.random.fold_in(rng, axis), (), 0, length) for axis, length in enumerate(drawn.shape)]
    main_axis = drawn.shape.index(max(drawn.shape))
    next_to = place[:main_axis] + [(place[main_axis] + 1) % drawn.shape[main_axis]] + place[main_axis + 1:]
    return drawn.at[tuple(place)].set(least).at[tuple(next_to)].set(largest)


def levels(stream_key, extent, cuts, low, high):
    factor_of, own = 1.0, jax.random.fold_in(stream_key, 6)
    for dim, blocks in cuts:
        heights = jnp.exp(jax.random.uniform(jax.random.fold_in(own, dim), (blocks,), jnp.float32, low / len(cuts), high / len(cuts)))
        factor_of = factor_of * jnp.repeat(heights, extent[dim] // blocks).reshape([-1 if axis == dim else 1 for axis in range(len(extent))])
    return factor_of


def centred(own_key, extent, width, limit, pieces=(), held_as=jnp.bfloat16):
    array = width * jax.random.normal(own_key, extent, jnp.float32)
    if pieces:
        array = array * levels(own_key, extent, pieces, -0.22, 0.18)
    return jnp.clip(array, -limit, limit).astype(held_as)


def setup_inputs(seed: int = 0) -> dict:
    seeds = jax.random.split(jax.random.key(seed), 10)
    return {
        "adjoint_in": centred(seeds[0], (OBJ, 2, NI, CELLS), 1.0, 6.0, ((0, 16), (2, 16)), jnp.float32),
        "checkpoint_store": draw_checkpoint_store(jax.random.fold_in(seeds[9], 71), 0),
        "interval": jax.random.randint(seeds[2], (1,), 0, SLOTS).astype(jnp.int32),
        "sea_mask": set_ends((jax.random.randint(seeds[3], (NI, CELLS), 0, 5) < 4).astype(jnp.int32), jax.random.fold_in(seeds[3], 1), 0, 1),
        "zonal_speed": jnp.clip(jax.random.uniform(seeds[4], (NI, CELLS), jnp.float32, -0.45, 0.45) * levels(seeds[4], (NI, CELLS), ((0, 16),), -0.4, 0.0), -0.45, 0.45),
        "mixing": jnp.clip(jnp.exp(math.log(0.2) - 2.3025851 * jax.random.uniform(seeds[5], (NI, CELLS), jnp.float32) ** levels(seeds[5], (NI, CELLS), ((0, 16),), -0.2, 0.2)), 0.02, 0.2),
        "piston": jnp.clip(jnp.exp(math.log(0.9) - 2.1972245 * jax.random.uniform(seeds[6], (NI, ROWS), jnp.float32) ** levels(seeds[6], (NI, ROWS), ((0, 16),), -0.2, 0.2)), 0.1, 0.9),
        "cell_area": jnp.clip(jnp.exp(math.log(50.0) - 2.3025851 * jax.random.uniform(seeds[7], (NI, ROWS), jnp.float32) ** levels(seeds[7], (NI, ROWS), ((0, 16),), -0.2, 0.2)), 5.0, 50.0),
        "region": set_ends(jax.random.randint(seeds[8], (NI, ROWS), 0, OBJ), jax.random.fold_in(seeds[8], 1), 0, OBJ - 1).astype(jnp.int32),
    }


DISSOCIATION_ONE = 1400.0
DISSOCIATION_TWO = 1.1
BORATE_CONSTANT = 2.5
BORON_TOTAL = 416.0
AIR_CARBON = 14.0
START_HYDROGEN = 2.0
ROW_DIFFUSION = 0.1

def chemistry(carbon, alkalinity, piston, surface_sea):
    hydrogen = jnp.full_like(carbon, START_HYDROGEN)
    for iteration in range(NEWTON):
        square = hydrogen * hydrogen
        denominator = square + DISSOCIATION_ONE * hydrogen + DISSOCIATION_ONE * DISSOCIATION_TWO
        carbonate = carbon * DISSOCIATION_ONE * (hydrogen + 2.0 * DISSOCIATION_TWO) / denominator
        borate = BORON_TOTAL * BORATE_CONSTANT / (hydrogen + BORATE_CONSTANT)
        derivative = -carbon * DISSOCIATION_ONE * (square + 4.0 * DISSOCIATION_TWO * hydrogen + DISSOCIATION_ONE * DISSOCIATION_TWO) / (denominator * denominator) - borate / (hydrogen + BORATE_CONSTANT)
        hydrogen = hydrogen - (carbonate + borate - alkalinity) / derivative
    square = hydrogen * hydrogen
    denominator = square + DISSOCIATION_ONE * hydrogen + DISSOCIATION_ONE * DISSOCIATION_TWO
    dissolved = carbon * square / denominator
    return surface_sea * piston * (AIR_CARBON - dissolved)

def forward_shift(source, offset):
    padding = jnp.zeros(source.shape[:-1] + (offset,), source.dtype)
    return jnp.concatenate([source[..., offset:], padding], axis=-1)

def backward_shift(source, offset):
    padding = jnp.zeros(source.shape[:-1] + (offset,), source.dtype)
    return jnp.concatenate([padding, source[..., :-offset]], axis=-1)

def column_weights(sea_float, mixing):
    cell_index = jnp.arange(LEVELS * ROWS, dtype=jnp.int32)
    row_open = (cell_index % ROWS < ROWS - 1).astype(jnp.float32)
    level_open = (cell_index // ROWS < LEVELS - 1).astype(jnp.float32)
    row_weight = ROW_DIFFUSION * row_open * sea_float * forward_shift(sea_float, 1)
    level_weight = mixing * level_open * sea_float * forward_shift(sea_float, ROWS)
    return (row_weight, level_weight)

def column_mix(source, row_weight, level_weight):
    row_flux = row_weight * (forward_shift(source, 1) - source)
    level_flux = level_weight * (forward_shift(source, ROWS) - source)
    return row_flux - backward_shift(row_flux, 1) + level_flux - backward_shift(level_flux, ROWS)

def zonal_weights(sea_float, sea_east, velocity):
    opened = sea_float * sea_east
    magnitude = jnp.abs(velocity)
    return jnp.stack([opened * (-velocity - magnitude) / 12.0, opened * (7.0 * velocity + 3.0 * magnitude) / 12.0, opened * (7.0 * velocity - 3.0 * magnitude) / 12.0, opened * (magnitude - velocity) / 12.0])

def advance(tracers, weights, row_weight, level_weight, piston, surface_sea):
    face_flux = weights[0] * jnp.roll(tracers, 1, axis=1) + weights[1] * tracers + weights[2] * jnp.roll(tracers, -1, axis=1) + weights[3] * jnp.roll(tracers, -2, axis=1)
    zonal_term = -(face_flux - jnp.roll(face_flux, 1, axis=1))
    transported = tracers + zonal_term + column_mix(tracers, row_weight, level_weight)
    uptake = chemistry(tracers[0, :, :ROWS], tracers[1, :, :ROWS], piston, surface_sea)
    surface_row = transported[0, :, :ROWS] + uptake
    carbon = jnp.concatenate([surface_row, transported[0, :, ROWS:]], axis=-1)
    return (jnp.stack([carbon, transported[1]]), uptake)

def reference(adjoint_in, checkpoint_store, interval, sea_mask, zonal_speed, mixing, piston, cell_area, region):
    sea_float = sea_mask.astype(jnp.float32)
    weights = zonal_weights(sea_float, jnp.roll(sea_float, -1, axis=0), zonal_speed)
    row_weight, level_weight = column_weights(sea_float, mixing)
    surface_sea = sea_float[:, :ROWS]
    position = interval[0] % N_OBJ * SLOT_DEV + interval[0] // N_OBJ
    initial = lax.dynamic_index_in_dim(checkpoint_store, position.astype(jnp.int32), 0, keepdims=False)

    def trajectory(tracers):
        tracers, uptake_first = advance(tracers, weights, row_weight, level_weight, piston, surface_sea)
        tracers, uptake_second = advance(tracers, weights, row_weight, level_weight, piston, surface_sea)
        return (tracers, jnp.stack([uptake_first, uptake_second]))
    _, pullback = jax.vjp(trajectory, initial)

    def sensitivity(objective_pair):
        cotangent, target = objective_pair
        seed_field = cell_area * (region == target).astype(jnp.float32)
        return pullback((cotangent, jnp.stack([seed_field, seed_field])))[0]
    targets = jnp.arange(OBJ, dtype=jnp.int32)
    return lax.map(sensitivity, (adjoint_in, targets))
```

```python
import jax
import jax.numpy as jnp
from jax import lax
from jax.sharding import PartitionSpec as P

ROWS = 32
LEVELS = 32
NEWTON = 4


DISSOCIATION_ONE = 1400.0
DISSOCIATION_TWO = 1.1
BORATE_CONSTANT = 2.5
BORON_TOTAL = 416.0
AIR_CARBON = 14.0
START_HYDROGEN = 2.0
ROW_DIFFUSION = 0.1


def padded(cells, sides, width):
    for axis, dim in sides:
        count = lax.axis_size(axis)
        head = lax.slice_in_dim(cells, 0, width, axis=dim)
        tail = lax.slice_in_dim(cells, cells.shape[dim] - width, cells.shape[dim], axis=dim)
        cells = jnp.concatenate(
            [
                lax.ppermute(tail, axis, [(i, (i + 1) % count) for i in range(count)]),
                cells,
                lax.ppermute(head, axis, [((i + 1) % count, i) for i in range(count)]),
            ],
            axis=dim,
        )
    return cells


def spread(value, axis, source):
    kept = jnp.where(lax.axis_index(axis) == source, value, 0).astype(value.dtype)
    return lax.psum(kept, axis)


def chemistry(carbon, alkalinity, piston, surface_sea):
    hydrogen = jnp.full_like(carbon, START_HYDROGEN)
    for iteration in range(NEWTON):
        square = hydrogen * hydrogen
        denominator = square + DISSOCIATION_ONE * hydrogen + DISSOCIATION_ONE * DISSOCIATION_TWO
        carbonate = carbon * DISSOCIATION_ONE * (hydrogen + 2.0 * DISSOCIATION_TWO) / denominator
        borate = BORON_TOTAL * BORATE_CONSTANT / (hydrogen + BORATE_CONSTANT)
        derivative = -carbon * DISSOCIATION_ONE * (
            square + 4.0 * DISSOCIATION_TWO * hydrogen + DISSOCIATION_ONE * DISSOCIATION_TWO
        ) / (denominator * denominator) - borate / (hydrogen + BORATE_CONSTANT)
        hydrogen = hydrogen - (carbonate + borate - alkalinity) / derivative
    square = hydrogen * hydrogen
    denominator = square + DISSOCIATION_ONE * hydrogen + DISSOCIATION_ONE * DISSOCIATION_TWO
    dissolved = carbon * square / denominator
    return surface_sea * piston * (AIR_CARBON - dissolved)


def forward_shift(source, offset):
    padding = jnp.zeros(source.shape[:-1] + (offset,), source.dtype)
    return jnp.concatenate([source[..., offset:], padding], axis=-1)


def backward_shift(source, offset):
    padding = jnp.zeros(source.shape[:-1] + (offset,), source.dtype)
    return jnp.concatenate([padding, source[..., :-offset]], axis=-1)


def column_weights(sea_float, mixing):
    cell_index = jnp.arange(LEVELS * ROWS, dtype=jnp.int32)
    row_open = (cell_index % ROWS < ROWS - 1).astype(jnp.float32)
    level_open = (cell_index // ROWS < LEVELS - 1).astype(jnp.float32)
    row_weight = ROW_DIFFUSION * row_open * sea_float * forward_shift(sea_float, 1)
    level_weight = mixing * level_open * sea_float * forward_shift(sea_float, ROWS)
    return (row_weight, level_weight)


def column_mix(source, row_weight, level_weight):
    row_flux = row_weight * (forward_shift(source, 1) - source)
    level_flux = level_weight * (forward_shift(source, ROWS) - source)
    return row_flux - backward_shift(row_flux, 1) + level_flux - backward_shift(level_flux, ROWS)


def zonal_weights(sea_float, sea_east, velocity):
    opened = sea_float * sea_east
    magnitude = jnp.abs(velocity)
    return jnp.stack(
        [
            opened * (-velocity - magnitude) / 12.0,
            opened * (7.0 * velocity + 3.0 * magnitude) / 12.0,
            opened * (7.0 * velocity - 3.0 * magnitude) / 12.0,
            opened * (magnitude - velocity) / 12.0,
        ]
    )


def trim_rim(source, keep_rim, outer_rim, dimension):
    length = source.shape[dimension] - 2 * outer_rim
    return lax.slice_in_dim(
        source, outer_rim - keep_rim, outer_rim + length + keep_rim, axis=dimension
    )


def surface_slopes(carbon, alkalinity, piston, surface_sea):

    def uptake_of(carbon_in, alkalinity_in):
        return chemistry(carbon_in, alkalinity_in, piston, surface_sea)

    uptake, pullback = jax.vjp(uptake_of, carbon, alkalinity)
    by_carbon, by_alkalinity = pullback(jnp.ones_like(carbon))
    return (uptake, jnp.stack([by_carbon, by_alkalinity]))


def advance_rim(extended, weights, row_weight, level_weight, uptake):
    length = extended.shape[1]
    face_flux = (
        weights[0, 1 : length - 2] * extended[:, 0 : length - 3]
        + weights[1, 1 : length - 2] * extended[:, 1 : length - 2]
        + weights[2, 1 : length - 2] * extended[:, 2 : length - 1]
        + weights[3, 1 : length - 2] * extended[:, 3:length]
    )
    interior = extended[:, 2 : length - 2]
    zonal_term = -(face_flux[:, 1:] - face_flux[:, :-1])
    transported = interior + zonal_term + column_mix(interior, row_weight, level_weight)
    surface_row = transported[0, :, :ROWS] + uptake
    carbon = jnp.concatenate([surface_row, transported[0, :, ROWS:]], axis=-1)
    return jnp.stack([carbon, transported[1]])


def retreat(extended, weights, row_weight, level_weight, slopes, objective_seeds):
    length = extended.shape[2]
    difference = extended[:, :, 1:] - extended[:, :, :-1]
    zonal_term = (
        weights[0, 3 : length - 1] * difference[:, :, 3 : length - 1]
        + weights[1, 2 : length - 2] * difference[:, :, 2 : length - 2]
        + weights[2, 1 : length - 3] * difference[:, :, 1 : length - 3]
        + weights[3, 0 : length - 4] * difference[:, :, 0 : length - 4]
    )
    interior = extended[:, :, 2 : length - 2]
    adjoint = interior + zonal_term + column_mix(interior, row_weight, level_weight)
    forcing = interior[:, 0, :, :ROWS] + objective_seeds
    surface = adjoint[..., :ROWS] + slopes[None] * forcing[:, None]
    return jnp.concatenate([surface, adjoint[..., ROWS:]], axis=-1)


def body(
    adjoint_in, checkpoint_store, interval, sea_mask, zonal_speed, mixing, piston, cell_area, region
):
    groups = adjoint_in.shape[0]
    cell_count = adjoint_in.shape[3]
    rim_depth = 4
    statics = jnp.concatenate(
        [
            sea_mask.astype(jnp.float32),
            zonal_speed,
            mixing,
            piston,
            cell_area,
            region.astype(jnp.float32),
        ],
        axis=1,
    )
    widened = padded(statics, (("tile", 0),), rim_depth)
    sea_wide = widened[:, :cell_count]
    speed_wide = widened[:, cell_count : 2 * cell_count]
    mixing_wide = widened[:, 2 * cell_count : 3 * cell_count]
    offset = 3 * cell_count
    piston_wide = widened[:, offset : offset + ROWS]
    area_wide = widened[:, offset + ROWS : offset + 2 * ROWS]
    region_wide = widened[:, offset + 2 * ROWS : offset + 3 * ROWS]
    sea_east = jnp.concatenate([sea_wide[1:], jnp.zeros_like(sea_wide[:1])], axis=0)
    weights = zonal_weights(sea_wide, sea_east, speed_wide)
    row_weight, level_weight = column_weights(sea_wide, mixing_wide)
    surface_sea = sea_wide[:, :ROWS]
    targets = (lax.axis_index("obj") * groups + jnp.arange(groups, dtype=jnp.int32)).astype(
        jnp.float32
    )
    objective_seeds = area_wide[None] * (region_wide[None] == targets[:, None, None]).astype(
        jnp.float32
    )
    owners = lax.axis_size("obj")
    owner_index = interval[0] % owners
    band = 2 * ROWS
    stored = lax.dynamic_index_in_dim(checkpoint_store, interval[0] // owners, 0, keepdims=False)
    stored = spread(stored[:, :, :band], "obj", owner_index)
    initial_wide = padded(stored, (("tile", 1),), rim_depth)
    inner_rim = 2
    piston_inner = trim_rim(piston_wide, inner_rim, rim_depth, 0)
    sea_inner = trim_rim(surface_sea, inner_rim, rim_depth, 0)
    initial_inner = trim_rim(initial_wide, inner_rim, rim_depth, 1)
    uptake_first, slopes_first = surface_slopes(
        initial_inner[0, :, :ROWS], initial_inner[1, :, :ROWS], piston_inner, sea_inner
    )
    following = advance_rim(
        initial_wide,
        weights[:, :, :band],
        trim_rim(row_weight, inner_rim, rim_depth, 0)[:, :band],
        trim_rim(level_weight, inner_rim, rim_depth, 0)[:, :band],
        uptake_first,
    )
    _, slopes_second = surface_slopes(
        following[0, :, :ROWS], following[1, :, :ROWS], piston_inner, sea_inner
    )
    extended = padded(adjoint_in, (("tile", 2),), rim_depth)
    middle = retreat(
        extended,
        weights,
        trim_rim(row_weight, inner_rim, rim_depth, 0),
        trim_rim(level_weight, inner_rim, rim_depth, 0),
        slopes_second,
        trim_rim(objective_seeds, inner_rim, rim_depth, 1),
    )
    return retreat(
        middle,
        trim_rim(weights, inner_rim, rim_depth, 1),
        trim_rim(row_weight, 0, rim_depth, 0),
        trim_rim(level_weight, 0, rim_depth, 0),
        trim_rim(slopes_first, 0, inner_rim, 1),
        trim_rim(objective_seeds, 0, rim_depth, 1),
    )


def solution(mesh):
    placed = (
        P("obj", None, "tile", None),
        P("obj", None, "tile", None),
        P(),
        P("tile", None),
        P("tile", None),
        P("tile", None),
        P("tile", None),
        P("tile", None),
        P("tile", None),
    )
    return jax.shard_map(
        body, mesh=mesh, in_specs=placed, out_specs=P("obj", None, "tile", None), check_vma=False
    )
```

```python
import jax
import jax.numpy as jnp
from jax import lax
from jax.sharding import PartitionSpec as P

ROWS = 32
LEVELS = 32
NEWTON = 4


DISSOCIATION_ONE = 1400.0
DISSOCIATION_TWO = 1.1
BORATE_CONSTANT = 2.5
BORON_TOTAL = 416.0
AIR_CARBON = 14.0
START_HYDROGEN = 2.0
ROW_DIFFUSION = 0.1


def padded(cells, sides, width):
    for axis, dim in sides:
        count = lax.axis_size(axis)
        head = lax.slice_in_dim(cells, 0, width, axis=dim)
        tail = lax.slice_in_dim(cells, cells.shape[dim] - width, cells.shape[dim], axis=dim)
        cells = jnp.concatenate(
            [
                lax.ppermute(tail, axis, [(i, (i + 1) % count) for i in range(count)]),
                cells,
                lax.ppermute(head, axis, [((i + 1) % count, i) for i in range(count)]),
            ],
            axis=dim,
        )
    return cells


def spread(value, axis, source):
    count = lax.axis_size(axis)
    rank = (lax.axis_index(axis) - source) % count
    reach = 1
    while reach < count:
        fan = min(4, -(-count // reach))
        received = value
        for k in range(1, fan):
            shift = k * reach
            moved = lax.ppermute(value, axis, [(i, (i + shift) % count) for i in range(count)])
            received = jnp.where((rank >= shift) & (rank < shift + reach), moved, received)
        value = received
        reach *= fan
    return value


def chemistry(carbon, alkalinity, piston, surface_sea):
    hydrogen = jnp.full_like(carbon, START_HYDROGEN)
    for iteration in range(NEWTON):
        square = hydrogen * hydrogen
        denominator = square + DISSOCIATION_ONE * hydrogen + DISSOCIATION_ONE * DISSOCIATION_TWO
        carbonate = carbon * DISSOCIATION_ONE * (hydrogen + 2.0 * DISSOCIATION_TWO) / denominator
        borate = BORON_TOTAL * BORATE_CONSTANT / (hydrogen + BORATE_CONSTANT)
        derivative = -carbon * DISSOCIATION_ONE * (
            square + 4.0 * DISSOCIATION_TWO * hydrogen + DISSOCIATION_ONE * DISSOCIATION_TWO
        ) / (denominator * denominator) - borate / (hydrogen + BORATE_CONSTANT)
        hydrogen = hydrogen - (carbonate + borate - alkalinity) / derivative
    square = hydrogen * hydrogen
    denominator = square + DISSOCIATION_ONE * hydrogen + DISSOCIATION_ONE * DISSOCIATION_TWO
    dissolved = carbon * square / denominator
    return surface_sea * piston * (AIR_CARBON - dissolved)


def forward_shift(source, offset):
    padding = jnp.zeros(source.shape[:-1] + (offset,), source.dtype)
    return jnp.concatenate([source[..., offset:], padding], axis=-1)


def backward_shift(source, offset):
    padding = jnp.zeros(source.shape[:-1] + (offset,), source.dtype)
    return jnp.concatenate([padding, source[..., :-offset]], axis=-1)


def column_weights(sea_float, mixing):
    cell_index = jnp.arange(LEVELS * ROWS, dtype=jnp.int32)
    row_open = (cell_index % ROWS < ROWS - 1).astype(jnp.float32)
    level_open = (cell_index // ROWS < LEVELS - 1).astype(jnp.float32)
    row_weight = ROW_DIFFUSION * row_open * sea_float * forward_shift(sea_float, 1)
    level_weight = mixing * level_open * sea_float * forward_shift(sea_float, ROWS)
    return (row_weight, level_weight)


def column_mix(source, row_weight, level_weight):
    row_flux = row_weight * (forward_shift(source, 1) - source)
    level_flux = level_weight * (forward_shift(source, ROWS) - source)
    return row_flux - backward_shift(row_flux, 1) + level_flux - backward_shift(level_flux, ROWS)


def zonal_weights(sea_float, sea_east, velocity):
    opened = sea_float * sea_east
    magnitude = jnp.abs(velocity)
    return jnp.stack(
        [
            opened * (-velocity - magnitude) / 12.0,
            opened * (7.0 * velocity + 3.0 * magnitude) / 12.0,
            opened * (7.0 * velocity - 3.0 * magnitude) / 12.0,
            opened * (magnitude - velocity) / 12.0,
        ]
    )


def trim_rim(source, keep_rim, outer_rim, dimension):
    length = source.shape[dimension] - 2 * outer_rim
    return lax.slice_in_dim(
        source, outer_rim - keep_rim, outer_rim + length + keep_rim, axis=dimension
    )


def surface_slopes(carbon, alkalinity, piston, surface_sea):

    def uptake_of(carbon_in, alkalinity_in):
        return chemistry(carbon_in, alkalinity_in, piston, surface_sea)

    uptake, pullback = jax.vjp(uptake_of, carbon, alkalinity)
    by_carbon, by_alkalinity = pullback(jnp.ones_like(carbon))
    return (uptake, jnp.stack([by_carbon, by_alkalinity]))


def advance_rim(extended, weights, row_weight, level_weight, uptake):
    length = extended.shape[1]
    face_flux = (
        weights[0, 1 : length - 2] * extended[:, 0 : length - 3]
        + weights[1, 1 : length - 2] * extended[:, 1 : length - 2]
        + weights[2, 1 : length - 2] * extended[:, 2 : length - 1]
        + weights[3, 1 : length - 2] * extended[:, 3:length]
    )
    interior = extended[:, 2 : length - 2]
    zonal_term = -(face_flux[:, 1:] - face_flux[:, :-1])
    transported = interior + zonal_term + column_mix(interior, row_weight, level_weight)
    surface_row = transported[0, :, :ROWS] + uptake
    carbon = jnp.concatenate([surface_row, transported[0, :, ROWS:]], axis=-1)
    return jnp.stack([carbon, transported[1]])


def retreat(extended, weights, row_weight, level_weight, slopes, objective_seeds):
    length = extended.shape[2]
    difference = extended[:, :, 1:] - extended[:, :, :-1]
    zonal_term = (
        weights[0, 3 : length - 1] * difference[:, :, 3 : length - 1]
        + weights[1, 2 : length - 2] * difference[:, :, 2 : length - 2]
        + weights[2, 1 : length - 3] * difference[:, :, 1 : length - 3]
        + weights[3, 0 : length - 4] * difference[:, :, 0 : length - 4]
    )
    interior = extended[:, :, 2 : length - 2]
    adjoint = interior + zonal_term + column_mix(interior, row_weight, level_weight)
    forcing = interior[:, 0, :, :ROWS] + objective_seeds
    surface = adjoint[..., :ROWS] + slopes[None] * forcing[:, None]
    return jnp.concatenate([surface, adjoint[..., ROWS:]], axis=-1)


def body(
    adjoint_in, checkpoint_store, interval, sea_mask, zonal_speed, mixing, piston, cell_area, region
):
    groups = adjoint_in.shape[0]
    cell_count = adjoint_in.shape[3]
    rim_depth = 4
    owners = lax.axis_size("obj")
    owner_index = interval[0] % owners
    band = 2 * ROWS
    stored = lax.dynamic_index_in_dim(checkpoint_store, interval[0] // owners, 0, keepdims=False)
    statics = jnp.concatenate(
        [
            stored[0, :, :band],
            stored[1, :, :band],
            sea_mask.astype(jnp.float32),
            zonal_speed,
            mixing,
            piston,
            cell_area,
            region.astype(jnp.float32),
        ],
        axis=1,
    )
    widened = padded(statics, (("tile", 0),), rim_depth)
    initial_wide = spread(
        jnp.stack([widened[:, :band], widened[:, band : 2 * band]]), "obj", owner_index
    )
    widened = widened[:, 2 * band :]
    sea_wide = widened[:, :cell_count]
    speed_wide = widened[:, cell_count : 2 * cell_count]
    mixing_wide = widened[:, 2 * cell_count : 3 * cell_count]
    offset = 3 * cell_count
    piston_wide = widened[:, offset : offset + ROWS]
    area_wide = widened[:, offset + ROWS : offset + 2 * ROWS]
    region_wide = widened[:, offset + 2 * ROWS : offset + 3 * ROWS]
    sea_east = jnp.concatenate([sea_wide[1:], jnp.zeros_like(sea_wide[:1])], axis=0)
    weights = zonal_weights(sea_wide, sea_east, speed_wide)
    row_weight, level_weight = column_weights(sea_wide, mixing_wide)
    surface_sea = sea_wide[:, :ROWS]
    targets = (lax.axis_index("obj") * groups + jnp.arange(groups, dtype=jnp.int32)).astype(
        jnp.float32
    )
    objective_seeds = area_wide[None] * (region_wide[None] == targets[:, None, None]).astype(
        jnp.float32
    )
    inner_rim = 2
    piston_inner = trim_rim(piston_wide, inner_rim, rim_depth, 0)
    sea_inner = trim_rim(surface_sea, inner_rim, rim_depth, 0)
    initial_inner = trim_rim(initial_wide, inner_rim, rim_depth, 1)
    uptake_first, slopes_first = surface_slopes(
        initial_inner[0, :, :ROWS], initial_inner[1, :, :ROWS], piston_inner, sea_inner
    )
    following = advance_rim(
        initial_wide,
        weights[:, :, :band],
        trim_rim(row_weight, inner_rim, rim_depth, 0)[:, :band],
        trim_rim(level_weight, inner_rim, rim_depth, 0)[:, :band],
        uptake_first,
    )
    _, slopes_second = surface_slopes(
        following[0, :, :ROWS], following[1, :, :ROWS], piston_inner, sea_inner
    )
    extended = padded(adjoint_in, (("tile", 2),), rim_depth)
    middle = retreat(
        extended,
        weights,
        trim_rim(row_weight, inner_rim, rim_depth, 0),
        trim_rim(level_weight, inner_rim, rim_depth, 0),
        slopes_second,
        trim_rim(objective_seeds, inner_rim, rim_depth, 1),
    )
    return retreat(
        middle,
        trim_rim(weights, inner_rim, rim_depth, 1),
        trim_rim(row_weight, 0, rim_depth, 0),
        trim_rim(level_weight, 0, rim_depth, 0),
        trim_rim(slopes_first, 0, inner_rim, 1),
        trim_rim(objective_seeds, 0, rim_depth, 1),
    )


def solution(mesh):
    placed = (
        P("obj", None, "tile", None),
        P("obj", None, "tile", None),
        P(),
        P("tile", None),
        P("tile", None),
        P("tile", None),
        P("tile", None),
        P("tile", None),
        P("tile", None),
    )
    return jax.shard_map(
        body, mesh=mesh, in_specs=placed, out_specs=P("obj", None, "tile", None), check_vma=False
    )
```

```python
import jax
import jax.numpy as jnp
from jax import lax
from jax.sharding import PartitionSpec as P
from jax.experimental import pallas as pl
from jax.experimental.pallas import tpu as pltpu

ROWS = 32
LEVELS = 32
NEWTON = 4


DISSOCIATION_ONE = 1400.0
DISSOCIATION_TWO = 1.1
BORATE_CONSTANT = 2.5
BORON_TOTAL = 416.0
AIR_CARBON = 14.0
START_HYDROGEN = 2.0
ROW_DIFFUSION = 0.1


def padded(cells, sides, width):
    for axis, dim in sides:
        count = lax.axis_size(axis)
        head = lax.slice_in_dim(cells, 0, width, axis=dim)
        tail = lax.slice_in_dim(cells, cells.shape[dim] - width, cells.shape[dim], axis=dim)
        cells = jnp.concatenate(
            [
                lax.ppermute(tail, axis, [(i, (i + 1) % count) for i in range(count)]),
                cells,
                lax.ppermute(head, axis, [((i + 1) % count, i) for i in range(count)]),
            ],
            axis=dim,
        )
    return cells


def spread(value, axis, source):
    count = lax.axis_size(axis)
    rank = (lax.axis_index(axis) - source) % count
    reach = 1
    while reach < count:
        fan = min(4, -(-count // reach))
        received = value
        for k in range(1, fan):
            shift = k * reach
            moved = lax.ppermute(value, axis, [(i, (i + shift) % count) for i in range(count)])
            received = jnp.where((rank >= shift) & (rank < shift + reach), moved, received)
        value = received
        reach *= fan
    return value


def chemistry(carbon, alkalinity, piston, surface_sea):
    hydrogen = jnp.full_like(carbon, START_HYDROGEN)
    for iteration in range(NEWTON):
        square = hydrogen * hydrogen
        denominator = square + DISSOCIATION_ONE * hydrogen + DISSOCIATION_ONE * DISSOCIATION_TWO
        carbonate = carbon * DISSOCIATION_ONE * (hydrogen + 2.0 * DISSOCIATION_TWO) / denominator
        borate = BORON_TOTAL * BORATE_CONSTANT / (hydrogen + BORATE_CONSTANT)
        derivative = -carbon * DISSOCIATION_ONE * (
            square + 4.0 * DISSOCIATION_TWO * hydrogen + DISSOCIATION_ONE * DISSOCIATION_TWO
        ) / (denominator * denominator) - borate / (hydrogen + BORATE_CONSTANT)
        hydrogen = hydrogen - (carbonate + borate - alkalinity) / derivative
    square = hydrogen * hydrogen
    denominator = square + DISSOCIATION_ONE * hydrogen + DISSOCIATION_ONE * DISSOCIATION_TWO
    dissolved = carbon * square / denominator
    return surface_sea * piston * (AIR_CARBON - dissolved)


def forward_shift(source, offset):
    padding = jnp.zeros(source.shape[:-1] + (offset,), source.dtype)
    return jnp.concatenate([source[..., offset:], padding], axis=-1)


def backward_shift(source, offset):
    padding = jnp.zeros(source.shape[:-1] + (offset,), source.dtype)
    return jnp.concatenate([padding, source[..., :-offset]], axis=-1)


def column_weights(sea_float, mixing):
    cell_index = jnp.arange(LEVELS * ROWS, dtype=jnp.int32)
    row_open = (cell_index % ROWS < ROWS - 1).astype(jnp.float32)
    level_open = (cell_index // ROWS < LEVELS - 1).astype(jnp.float32)
    row_weight = ROW_DIFFUSION * row_open * sea_float * forward_shift(sea_float, 1)
    level_weight = mixing * level_open * sea_float * forward_shift(sea_float, ROWS)
    return (row_weight, level_weight)


def column_mix(source, row_weight, level_weight):
    row_flux = row_weight * (forward_shift(source, 1) - source)
    level_flux = level_weight * (forward_shift(source, ROWS) - source)
    return row_flux - backward_shift(row_flux, 1) + level_flux - backward_shift(level_flux, ROWS)


def zonal_weights(sea_float, sea_east, velocity):
    opened = sea_float * sea_east
    magnitude = jnp.abs(velocity)
    return jnp.stack(
        [
            opened * (-velocity - magnitude) / 12.0,
            opened * (7.0 * velocity + 3.0 * magnitude) / 12.0,
            opened * (7.0 * velocity - 3.0 * magnitude) / 12.0,
            opened * (magnitude - velocity) / 12.0,
        ]
    )


def trim_rim(source, keep_rim, outer_rim, dimension):
    length = source.shape[dimension] - 2 * outer_rim
    return lax.slice_in_dim(
        source, outer_rim - keep_rim, outer_rim + length + keep_rim, axis=dimension
    )


def surface_slopes(carbon, alkalinity, piston, surface_sea):

    def uptake_of(carbon_in, alkalinity_in):
        return chemistry(carbon_in, alkalinity_in, piston, surface_sea)

    uptake, pullback = jax.vjp(uptake_of, carbon, alkalinity)
    by_carbon, by_alkalinity = pullback(jnp.ones_like(carbon))
    return (uptake, jnp.stack([by_carbon, by_alkalinity]))


def advance_rim(extended, weights, row_weight, level_weight, uptake):
    length = extended.shape[1]
    face_flux = (
        weights[0, 1 : length - 2] * extended[:, 0 : length - 3]
        + weights[1, 1 : length - 2] * extended[:, 1 : length - 2]
        + weights[2, 1 : length - 2] * extended[:, 2 : length - 1]
        + weights[3, 1 : length - 2] * extended[:, 3:length]
    )
    interior = extended[:, 2 : length - 2]
    zonal_term = -(face_flux[:, 1:] - face_flux[:, :-1])
    transported = interior + zonal_term + column_mix(interior, row_weight, level_weight)
    surface_row = transported[0, :, :ROWS] + uptake
    carbon = jnp.concatenate([surface_row, transported[0, :, ROWS:]], axis=-1)
    return jnp.stack([carbon, transported[1]])


def retreat(extended, weights, row_weight, level_weight, slopes, objective_seeds):
    length = extended.shape[2]
    difference = extended[:, :, 1:] - extended[:, :, :-1]
    zonal_term = (
        weights[0, 3 : length - 1] * difference[:, :, 3 : length - 1]
        + weights[1, 2 : length - 2] * difference[:, :, 2 : length - 2]
        + weights[2, 1 : length - 3] * difference[:, :, 1 : length - 3]
        + weights[3, 0 : length - 4] * difference[:, :, 0 : length - 4]
    )
    interior = extended[:, :, 2 : length - 2]
    adjoint = interior + zonal_term + column_mix(interior, row_weight, level_weight)
    forcing = interior[:, 0, :, :ROWS] + objective_seeds
    surface = adjoint[..., :ROWS] + slopes[None] * forcing[:, None]
    return jnp.concatenate([surface, adjoint[..., ROWS:]], axis=-1)


SPAN = 48
ORIGIN = 16


def halves(cells, axis, dim, width):
    count = lax.axis_size(axis)
    head = lax.slice_in_dim(cells, 0, width, axis=dim)
    tail = lax.slice_in_dim(cells, cells.shape[dim] - width, cells.shape[dim], axis=dim)
    west = lax.ppermute(tail, axis, [(i, (i + 1) % count) for i in range(count)])
    east = lax.ppermute(head, axis, [((i + 1) % count, i) for i in range(count)])
    return west, east


def placed_rows(source, first, total=SPAN):
    pad = [(0, 0)] * source.ndim
    pad[-2] = (first, total - first - source.shape[-2])
    return jnp.pad(source, pad)


def lanes_to(source, width):
    pad = [(0, 0)] * source.ndim
    pad[-1] = (0, width - source.shape[-1])
    return jnp.pad(source, pad)


def retreat_kernel(center_ref, west_ref, east_ref, w_ref, s_ref, seed_ref, out_ref, e_ref, f_ref):
    local = center_ref.shape[2]
    width = center_ref.shape[3]
    rim = west_ref.shape[2]
    e_ref[:, ORIGIN : ORIGIN + local, :] = center_ref[0]
    e_ref[:, ORIGIN - rim : ORIGIN, :] = west_ref[0]
    e_ref[:, ORIGIN + local : ORIGIN + local + rim, :] = east_ref[0]

    def block(src, r, t, stage):
        x_m2 = src[t, r - 2 : r + 6, :]
        x_m1 = src[t, r - 1 : r + 7, :]
        x_0 = src[t, r : r + 8, :]
        x_p1 = src[t, r + 1 : r + 9, :]
        x_p2 = src[t, r + 2 : r + 10, :]
        zonal = (
            w_ref[0, r : r + 8, :] * (x_p2 - x_p1)
            + w_ref[1, r : r + 8, :] * (x_p1 - x_0)
            + w_ref[2, r : r + 8, :] * (x_0 - x_m1)
            + w_ref[3, r : r + 8, :] * (x_m1 - x_m2)
        )
        row_flux = w_ref[4, r : r + 8, :] * (pltpu.roll(x_0, width - 1, 1) - x_0)
        level_flux = w_ref[5, r : r + 8, :] * (pltpu.roll(x_0, width - ROWS, 1) - x_0)
        mix = row_flux - pltpu.roll(row_flux, 1, 1) + level_flux - pltpu.roll(level_flux, ROWS, 1)
        adjoint = x_0 + zonal + mix
        forcing = src[0, r : r + 8, 0:128] + seed_ref[0, r : r + 8, :]
        head = adjoint[:, 0:128] + s_ref[stage, t, r : r + 8, :] * forcing
        return head, adjoint[:, 128:]

    for r in range(ORIGIN - 8, ORIGIN + local + 8, 8):
        for t in range(2):
            head, rest = block(e_ref, r, t, 0)
            f_ref[t, r : r + 8, 0:128] = head
            f_ref[t, r : r + 8, 128:] = rest
    for r in range(ORIGIN, ORIGIN + local, 8):
        for t in range(2):
            head, rest = block(f_ref, r, t, 1)
            out_ref[0, t, r - ORIGIN : r - ORIGIN + 8, 0:128] = head
            out_ref[0, t, r - ORIGIN : r - ORIGIN + 8, 128:] = rest


def two_retreats(center, west, east, stencil, slopes, seeds):
    groups, tracers, local, width = center.shape
    rim = west.shape[2]
    return pl.pallas_call(
        retreat_kernel,
        out_shape=jax.ShapeDtypeStruct(center.shape, center.dtype),
        grid=(groups,),
        in_specs=[
            pl.BlockSpec((1, tracers, local, width), lambda g: (g, 0, 0, 0)),
            pl.BlockSpec((1, tracers, rim, width), lambda g: (g, 0, 0, 0)),
            pl.BlockSpec((1, tracers, rim, width), lambda g: (g, 0, 0, 0)),
            pl.BlockSpec(stencil.shape, lambda g: (0, 0, 0)),
            pl.BlockSpec(slopes.shape, lambda g: (0, 0, 0, 0)),
            pl.BlockSpec((1,) + seeds.shape[1:], lambda g: (g, 0, 0)),
        ],
        out_specs=pl.BlockSpec((1, tracers, local, width), lambda g: (g, 0, 0, 0)),
        scratch_shapes=[
            pltpu.VMEM((tracers, SPAN, width), jnp.float32),
            pltpu.VMEM((tracers, SPAN, width), jnp.float32),
        ],
    )(center, west, east, stencil, slopes, seeds)


def body(
    adjoint_in, checkpoint_store, interval, sea_mask, zonal_speed, mixing, piston, cell_area, region
):
    groups = adjoint_in.shape[0]
    cell_count = adjoint_in.shape[3]
    rim_depth = 4
    owners = lax.axis_size("obj")
    owner_index = interval[0] % owners
    band = 2 * ROWS
    stored = lax.dynamic_index_in_dim(checkpoint_store, interval[0] // owners, 0, keepdims=False)
    statics = jnp.concatenate(
        [
            stored[0, :, :band],
            stored[1, :, :band],
            sea_mask.astype(jnp.float32),
            zonal_speed,
            mixing,
            piston,
            cell_area,
            region.astype(jnp.float32),
        ],
        axis=1,
    )
    widened = padded(statics, (("tile", 0),), rim_depth)
    initial_wide = spread(
        jnp.stack([widened[:, :band], widened[:, band : 2 * band]]), "obj", owner_index
    )
    widened = widened[:, 2 * band :]
    sea_wide = widened[:, :cell_count]
    speed_wide = widened[:, cell_count : 2 * cell_count]
    mixing_wide = widened[:, 2 * cell_count : 3 * cell_count]
    offset = 3 * cell_count
    piston_wide = widened[:, offset : offset + ROWS]
    area_wide = widened[:, offset + ROWS : offset + 2 * ROWS]
    region_wide = widened[:, offset + 2 * ROWS : offset + 3 * ROWS]
    sea_east = jnp.concatenate([sea_wide[1:], jnp.zeros_like(sea_wide[:1])], axis=0)
    weights = zonal_weights(sea_wide, sea_east, speed_wide)
    row_weight, level_weight = column_weights(sea_wide, mixing_wide)
    surface_sea = sea_wide[:, :ROWS]
    targets = (lax.axis_index("obj") * groups + jnp.arange(groups, dtype=jnp.int32)).astype(
        jnp.float32
    )
    objective_seeds = area_wide[None] * (region_wide[None] == targets[:, None, None]).astype(
        jnp.float32
    )
    inner_rim = 2
    piston_inner = trim_rim(piston_wide, inner_rim, rim_depth, 0)
    sea_inner = trim_rim(surface_sea, inner_rim, rim_depth, 0)
    initial_inner = trim_rim(initial_wide, inner_rim, rim_depth, 1)
    uptake_first, slopes_first = surface_slopes(
        initial_inner[0, :, :ROWS], initial_inner[1, :, :ROWS], piston_inner, sea_inner
    )
    following = advance_rim(
        initial_wide,
        weights[:, :, :band],
        trim_rim(row_weight, inner_rim, rim_depth, 0)[:, :band],
        trim_rim(level_weight, inner_rim, rim_depth, 0)[:, :band],
        uptake_first,
    )
    _, slopes_second = surface_slopes(
        following[0, :, :ROWS], following[1, :, :ROWS], piston_inner, sea_inner
    )
    west, east = halves(adjoint_in, "tile", 2, rim_depth)
    first = ORIGIN - rim_depth
    stencil = jnp.stack(
        [
            placed_rows(weights[0], first - 1),
            placed_rows(weights[1], first),
            placed_rows(weights[2], first + 1),
            placed_rows(weights[3], first + 2),
            placed_rows(row_weight, first),
            placed_rows(level_weight, first),
        ]
    )
    slopes = lanes_to(
        jnp.stack(
            [
                placed_rows(slopes_second, ORIGIN - inner_rim),
                placed_rows(trim_rim(slopes_first, 0, inner_rim, 1), ORIGIN),
            ]
        ),
        128,
    )
    seeds = lanes_to(placed_rows(objective_seeds, first), 128)
    return two_retreats(adjoint_in, west, east, stencil, slopes, seeds)


def solution(mesh):
    placed = (
        P("obj", None, "tile", None),
        P("obj", None, "tile", None),
        P(),
        P("tile", None),
        P("tile", None),
        P("tile", None),
        P("tile", None),
        P("tile", None),
        P("tile", None),
    )
    return jax.shard_map(
        body, mesh=mesh, in_specs=placed, out_specs=P("obj", None, "tile", None), check_vma=False
    )
```

```python
import jax
import jax.numpy as jnp
from jax import lax
from jax.sharding import PartitionSpec as P
from jax.experimental import pallas as pl
from jax.experimental.pallas import tpu as pltpu

ROWS = 32
LEVELS = 32
NEWTON = 4


DISSOCIATION_ONE = 1400.0
DISSOCIATION_TWO = 1.1
BORATE_CONSTANT = 2.5
BORON_TOTAL = 416.0
AIR_CARBON = 14.0
START_HYDROGEN = 2.0
ROW_DIFFUSION = 0.1


def padded(cells, sides, width):
    for axis, dim in sides:
        count = lax.axis_size(axis)
        head = lax.slice_in_dim(cells, 0, width, axis=dim)
        tail = lax.slice_in_dim(cells, cells.shape[dim] - width, cells.shape[dim], axis=dim)
        cells = jnp.concatenate(
            [
                lax.ppermute(tail, axis, [(i, (i + 1) % count) for i in range(count)]),
                cells,
                lax.ppermute(head, axis, [((i + 1) % count, i) for i in range(count)]),
            ],
            axis=dim,
        )
    return cells


def spread(value, axis, source):
    count = lax.axis_size(axis)
    top = count // 2
    if count < 2 or count & (count - 1):
        kept = jnp.where(lax.axis_index(axis) == source, value, 0).astype(value.dtype)
        return lax.psum(kept, axis)
    rank = jnp.bitwise_xor(lax.axis_index(axis), source)
    moved = lax.ppermute(value, axis, [(i, i ^ top) for i in range(count)])
    value = jnp.where(rank == top, moved, value)
    low = rank & (top - 1)
    received = value
    for mask in range(1, top):
        moved = lax.ppermute(value, axis, [(i, i ^ mask) for i in range(count)])
        received = jnp.where(low == mask, moved, received)
    return received


def chemistry(carbon, alkalinity, piston, surface_sea):
    hydrogen = jnp.full_like(carbon, START_HYDROGEN)
    for iteration in range(NEWTON):
        square = hydrogen * hydrogen
        denominator = square + DISSOCIATION_ONE * hydrogen + DISSOCIATION_ONE * DISSOCIATION_TWO
        carbonate = carbon * DISSOCIATION_ONE * (hydrogen + 2.0 * DISSOCIATION_TWO) / denominator
        borate = BORON_TOTAL * BORATE_CONSTANT / (hydrogen + BORATE_CONSTANT)
        derivative = -carbon * DISSOCIATION_ONE * (
            square + 4.0 * DISSOCIATION_TWO * hydrogen + DISSOCIATION_ONE * DISSOCIATION_TWO
        ) / (denominator * denominator) - borate / (hydrogen + BORATE_CONSTANT)
        hydrogen = hydrogen - (carbonate + borate - alkalinity) / derivative
    square = hydrogen * hydrogen
    denominator = square + DISSOCIATION_ONE * hydrogen + DISSOCIATION_ONE * DISSOCIATION_TWO
    dissolved = carbon * square / denominator
    return surface_sea * piston * (AIR_CARBON - dissolved)


def forward_shift(source, offset):
    padding = jnp.zeros(source.shape[:-1] + (offset,), source.dtype)
    return jnp.concatenate([source[..., offset:], padding], axis=-1)


def backward_shift(source, offset):
    padding = jnp.zeros(source.shape[:-1] + (offset,), source.dtype)
    return jnp.concatenate([padding, source[..., :-offset]], axis=-1)


def column_weights(sea_float, mixing):
    cell_index = jnp.arange(LEVELS * ROWS, dtype=jnp.int32)
    row_open = (cell_index % ROWS < ROWS - 1).astype(jnp.float32)
    level_open = (cell_index // ROWS < LEVELS - 1).astype(jnp.float32)
    row_weight = ROW_DIFFUSION * row_open * sea_float * forward_shift(sea_float, 1)
    level_weight = mixing * level_open * sea_float * forward_shift(sea_float, ROWS)
    return (row_weight, level_weight)


def column_mix(source, row_weight, level_weight):
    row_flux = row_weight * (forward_shift(source, 1) - source)
    level_flux = level_weight * (forward_shift(source, ROWS) - source)
    return row_flux - backward_shift(row_flux, 1) + level_flux - backward_shift(level_flux, ROWS)


def zonal_weights(sea_float, sea_east, velocity):
    opened = sea_float * sea_east
    magnitude = jnp.abs(velocity)
    return jnp.stack(
        [
            opened * (-velocity - magnitude) / 12.0,
            opened * (7.0 * velocity + 3.0 * magnitude) / 12.0,
            opened * (7.0 * velocity - 3.0 * magnitude) / 12.0,
            opened * (magnitude - velocity) / 12.0,
        ]
    )


def trim_rim(source, keep_rim, outer_rim, dimension):
    length = source.shape[dimension] - 2 * outer_rim
    return lax.slice_in_dim(
        source, outer_rim - keep_rim, outer_rim + length + keep_rim, axis=dimension
    )


def surface_slopes(carbon, alkalinity, piston, surface_sea):

    def uptake_of(carbon_in, alkalinity_in):
        return chemistry(carbon_in, alkalinity_in, piston, surface_sea)

    uptake, pullback = jax.vjp(uptake_of, carbon, alkalinity)
    by_carbon, by_alkalinity = pullback(jnp.ones_like(carbon))
    return (uptake, jnp.stack([by_carbon, by_alkalinity]))


def advance_rim(extended, weights, row_weight, level_weight, uptake):
    length = extended.shape[1]
    face_flux = (
        weights[0, 1 : length - 2] * extended[:, 0 : length - 3]
        + weights[1, 1 : length - 2] * extended[:, 1 : length - 2]
        + weights[2, 1 : length - 2] * extended[:, 2 : length - 1]
        + weights[3, 1 : length - 2] * extended[:, 3:length]
    )
    interior = extended[:, 2 : length - 2]
    zonal_term = -(face_flux[:, 1:] - face_flux[:, :-1])
    transported = interior + zonal_term + column_mix(interior, row_weight, level_weight)
    surface_row = transported[0, :, :ROWS] + uptake
    carbon = jnp.concatenate([surface_row, transported[0, :, ROWS:]], axis=-1)
    return jnp.stack([carbon, transported[1]])


def retreat(extended, weights, row_weight, level_weight, slopes, objective_seeds):
    length = extended.shape[2]
    difference = extended[:, :, 1:] - extended[:, :, :-1]
    zonal_term = (
        weights[0, 3 : length - 1] * difference[:, :, 3 : length - 1]
        + weights[1, 2 : length - 2] * difference[:, :, 2 : length - 2]
        + weights[2, 1 : length - 3] * difference[:, :, 1 : length - 3]
        + weights[3, 0 : length - 4] * difference[:, :, 0 : length - 4]
    )
    interior = extended[:, :, 2 : length - 2]
    adjoint = interior + zonal_term + column_mix(interior, row_weight, level_weight)
    forcing = interior[:, 0, :, :ROWS] + objective_seeds
    surface = adjoint[..., :ROWS] + slopes[None] * forcing[:, None]
    return jnp.concatenate([surface, adjoint[..., ROWS:]], axis=-1)


SPAN = 40
ORIGIN = 10


def halves(cells, axis, dim, width):
    count = lax.axis_size(axis)
    head = lax.slice_in_dim(cells, 0, width, axis=dim)
    tail = lax.slice_in_dim(cells, cells.shape[dim] - width, cells.shape[dim], axis=dim)
    west = lax.ppermute(tail, axis, [(i, (i + 1) % count) for i in range(count)])
    east = lax.ppermute(head, axis, [((i + 1) % count, i) for i in range(count)])
    return west, east


def placed_rows(source, first, total=SPAN):
    pad = [(0, 0)] * source.ndim
    pad[-2] = (first, total - first - source.shape[-2])
    return jnp.pad(source, pad)


def lanes_to(source, width):
    pad = [(0, 0)] * source.ndim
    pad[-1] = (0, width - source.shape[-1])
    return jnp.pad(source, pad)


def retreat_kernel(center_ref, west_ref, east_ref, w_ref, s_ref, seed_ref, out_ref, e_ref, f_ref):
    local = center_ref.shape[2]
    width = center_ref.shape[3]
    rim = west_ref.shape[2]
    e_ref[:, ORIGIN : ORIGIN + local, :] = center_ref[0]
    e_ref[:, ORIGIN - rim : ORIGIN, :] = west_ref[0]
    e_ref[:, ORIGIN + local : ORIGIN + local + rim, :] = east_ref[0]

    def block(src, r, t, stage):
        x_m2 = src[t, r - 2 : r + 6, :]
        x_m1 = src[t, r - 1 : r + 7, :]
        x_0 = src[t, r : r + 8, :]
        x_p1 = src[t, r + 1 : r + 9, :]
        x_p2 = src[t, r + 2 : r + 10, :]
        zonal = (
            w_ref[0, r : r + 8, :] * (x_p2 - x_p1)
            + w_ref[1, r : r + 8, :] * (x_p1 - x_0)
            + w_ref[2, r : r + 8, :] * (x_0 - x_m1)
            + w_ref[3, r : r + 8, :] * (x_m1 - x_m2)
        )
        row_flux = w_ref[4, r : r + 8, :] * (pltpu.roll(x_0, width - 1, 1) - x_0)
        level_flux = w_ref[5, r : r + 8, :] * (pltpu.roll(x_0, width - ROWS, 1) - x_0)
        mix = row_flux - pltpu.roll(row_flux, 1, 1) + level_flux - pltpu.roll(level_flux, ROWS, 1)
        adjoint = x_0 + zonal + mix
        forcing = src[0, r : r + 8, 0:128] + seed_ref[0, r : r + 8, :]
        head = adjoint[:, 0:128] + s_ref[stage, t, r : r + 8, :] * forcing
        return head, adjoint[:, 128:]

    for r in range(ORIGIN - 2, ORIGIN + local + 2, 8):
        for t in range(2):
            head, rest = block(e_ref, r, t, 0)
            f_ref[t, r : r + 8, 0:128] = head
            f_ref[t, r : r + 8, 128:] = rest
    for r in range(ORIGIN, ORIGIN + local, 8):
        for t in range(2):
            head, rest = block(f_ref, r, t, 1)
            out_ref[0, t, r - ORIGIN : r - ORIGIN + 8, 0:128] = head
            out_ref[0, t, r - ORIGIN : r - ORIGIN + 8, 128:] = rest


def two_retreats(center, west, east, stencil, slopes, seeds):
    groups, tracers, local, width = center.shape
    rim = west.shape[2]
    return pl.pallas_call(
        retreat_kernel,
        out_shape=jax.ShapeDtypeStruct(center.shape, center.dtype),
        grid=(groups,),
        in_specs=[
            pl.BlockSpec((1, tracers, local, width), lambda g: (g, 0, 0, 0)),
            pl.BlockSpec((1, tracers, rim, width), lambda g: (g, 0, 0, 0)),
            pl.BlockSpec((1, tracers, rim, width), lambda g: (g, 0, 0, 0)),
            pl.BlockSpec(stencil.shape, lambda g: (0, 0, 0)),
            pl.BlockSpec(slopes.shape, lambda g: (0, 0, 0, 0)),
            pl.BlockSpec((1,) + seeds.shape[1:], lambda g: (g, 0, 0)),
        ],
        out_specs=pl.BlockSpec((1, tracers, local, width), lambda g: (g, 0, 0, 0)),
        scratch_shapes=[
            pltpu.VMEM((tracers, SPAN, width), jnp.float32),
            pltpu.VMEM((tracers, SPAN, width), jnp.float32),
        ],
    )(center, west, east, stencil, slopes, seeds)


def body(
    adjoint_in, checkpoint_store, interval, sea_mask, zonal_speed, mixing, piston, cell_area, region
):
    groups = adjoint_in.shape[0]
    cell_count = adjoint_in.shape[3]
    rim_depth = 4
    owners = lax.axis_size("obj")
    owner_index = interval[0] % owners
    band = 2 * ROWS
    stored = lax.dynamic_index_in_dim(checkpoint_store, interval[0] // owners, 0, keepdims=False)
    statics = jnp.concatenate(
        [
            stored[0, :, :band],
            stored[1, :, :band],
            sea_mask.astype(jnp.float32),
            zonal_speed,
            mixing,
            piston,
            cell_area,
            region.astype(jnp.float32),
        ],
        axis=1,
    )
    widened = padded(statics, (("tile", 0),), rim_depth)
    initial_wide = spread(
        jnp.stack([widened[:, :band], widened[:, band : 2 * band]]), "obj", owner_index
    )
    widened = widened[:, 2 * band :]
    sea_wide = widened[:, :cell_count]
    speed_wide = widened[:, cell_count : 2 * cell_count]
    mixing_wide = widened[:, 2 * cell_count : 3 * cell_count]
    offset = 3 * cell_count
    piston_wide = widened[:, offset : offset + ROWS]
    area_wide = widened[:, offset + ROWS : offset + 2 * ROWS]
    region_wide = widened[:, offset + 2 * ROWS : offset + 3 * ROWS]
    sea_east = jnp.concatenate([sea_wide[1:], jnp.zeros_like(sea_wide[:1])], axis=0)
    weights = zonal_weights(sea_wide, sea_east, speed_wide)
    row_weight, level_weight = column_weights(sea_wide, mixing_wide)
    surface_sea = sea_wide[:, :ROWS]
    targets = (lax.axis_index("obj") * groups + jnp.arange(groups, dtype=jnp.int32)).astype(
        jnp.float32
    )
    objective_seeds = area_wide[None] * (region_wide[None] == targets[:, None, None]).astype(
        jnp.float32
    )
    inner_rim = 2
    piston_inner = trim_rim(piston_wide, inner_rim, rim_depth, 0)
    sea_inner = trim_rim(surface_sea, inner_rim, rim_depth, 0)
    initial_inner = trim_rim(initial_wide, inner_rim, rim_depth, 1)
    uptake_first, slopes_first = surface_slopes(
        initial_inner[0, :, :ROWS], initial_inner[1, :, :ROWS], piston_inner, sea_inner
    )
    following = advance_rim(
        initial_wide,
        weights[:, :, :band],
        trim_rim(row_weight, inner_rim, rim_depth, 0)[:, :band],
        trim_rim(level_weight, inner_rim, rim_depth, 0)[:, :band],
        uptake_first,
    )
    _, slopes_second = surface_slopes(
        following[0, :, :ROWS], following[1, :, :ROWS], piston_inner, sea_inner
    )
    west, east = halves(adjoint_in, "tile", 2, rim_depth)
    first = ORIGIN - rim_depth
    stencil = jnp.stack(
        [
            placed_rows(weights[0], first - 1),
            placed_rows(weights[1], first),
            placed_rows(weights[2], first + 1),
            placed_rows(weights[3], first + 2),
            placed_rows(row_weight, first),
            placed_rows(level_weight, first),
        ]
    )
    slopes = lanes_to(
        jnp.stack(
            [
                placed_rows(slopes_second, ORIGIN - inner_rim),
                placed_rows(trim_rim(slopes_first, 0, inner_rim, 1), ORIGIN),
            ]
        ),
        128,
    )
    seeds = lanes_to(placed_rows(objective_seeds, first), 128)
    return two_retreats(adjoint_in, west, east, stencil, slopes, seeds)


def solution(mesh):
    placed = (
        P("obj", None, "tile", None),
        P("obj", None, "tile", None),
        P(),
        P("tile", None),
        P("tile", None),
        P("tile", None),
        P("tile", None),
        P("tile", None),
        P("tile", None),
    )
    return jax.shard_map(
        body, mesh=mesh, in_specs=placed, out_specs=P("obj", None, "tile", None), check_vma=False
    )
```

```python
import jax
import jax.numpy as jnp
from jax import lax
from jax.sharding import PartitionSpec as P
from jax.experimental import pallas as pl
from jax.experimental.pallas import tpu as pltpu

ROWS = 32
LEVELS = 32
NEWTON = 4


DISSOCIATION_ONE = 1400.0
DISSOCIATION_TWO = 1.1
BORATE_CONSTANT = 2.5
BORON_TOTAL = 416.0
AIR_CARBON = 14.0
START_HYDROGEN = 2.0
ROW_DIFFUSION = 0.1


def padded(cells, sides, width):
    for axis, dim in sides:
        count = lax.axis_size(axis)
        head = lax.slice_in_dim(cells, 0, width, axis=dim)
        tail = lax.slice_in_dim(cells, cells.shape[dim] - width, cells.shape[dim], axis=dim)
        cells = jnp.concatenate(
            [
                lax.ppermute(tail, axis, [(i, (i + 1) % count) for i in range(count)]),
                cells,
                lax.ppermute(head, axis, [((i + 1) % count, i) for i in range(count)]),
            ],
            axis=dim,
        )
    return cells


def spread(value, axis, source):
    count = lax.axis_size(axis)
    top = count // 2
    if count < 2 or count & (count - 1):
        kept = jnp.where(lax.axis_index(axis) == source, value, 0).astype(value.dtype)
        return lax.psum(kept, axis)
    rank = jnp.bitwise_xor(lax.axis_index(axis), source)
    moved = lax.ppermute(value, axis, [(i, i ^ top) for i in range(count)])
    value = jnp.where(rank == top, moved, value)
    low = rank & (top - 1)
    received = value
    for mask in range(1, top):
        moved = lax.ppermute(value, axis, [(i, i ^ mask) for i in range(count)])
        received = jnp.where(low == mask, moved, received)
    return received


def chemistry(carbon, alkalinity, piston, surface_sea):
    hydrogen = jnp.full_like(carbon, START_HYDROGEN)
    for _ in range(NEWTON):
        square = hydrogen * hydrogen
        denominator = square + DISSOCIATION_ONE * hydrogen + DISSOCIATION_ONE * DISSOCIATION_TWO
        carbonate = carbon * DISSOCIATION_ONE * (hydrogen + 2.0 * DISSOCIATION_TWO) / denominator
        borate = BORON_TOTAL * BORATE_CONSTANT / (hydrogen + BORATE_CONSTANT)
        derivative = -carbon * DISSOCIATION_ONE * (
            square + 4.0 * DISSOCIATION_TWO * hydrogen + DISSOCIATION_ONE * DISSOCIATION_TWO
        ) / (denominator * denominator) - borate / (hydrogen + BORATE_CONSTANT)
        hydrogen = hydrogen - (carbonate + borate - alkalinity) / derivative
    square = hydrogen * hydrogen
    denominator = square + DISSOCIATION_ONE * hydrogen + DISSOCIATION_ONE * DISSOCIATION_TWO
    dissolved = carbon * square / denominator
    return surface_sea * piston * (AIR_CARBON - dissolved)


def forward_shift(source, offset):
    padding = jnp.zeros(source.shape[:-1] + (offset,), source.dtype)
    return jnp.concatenate([source[..., offset:], padding], axis=-1)


def backward_shift(source, offset):
    padding = jnp.zeros(source.shape[:-1] + (offset,), source.dtype)
    return jnp.concatenate([padding, source[..., :-offset]], axis=-1)


def column_weights(sea_float, mixing):
    cell_index = jnp.arange(LEVELS * ROWS, dtype=jnp.int32)
    row_open = (cell_index % ROWS < ROWS - 1).astype(jnp.float32)
    level_open = (cell_index // ROWS < LEVELS - 1).astype(jnp.float32)
    row_weight = ROW_DIFFUSION * row_open * sea_float * forward_shift(sea_float, 1)
    level_weight = mixing * level_open * sea_float * forward_shift(sea_float, ROWS)
    return (row_weight, level_weight)


def column_mix(source, row_weight, level_weight):
    row_flux = row_weight * (forward_shift(source, 1) - source)
    level_flux = level_weight * (forward_shift(source, ROWS) - source)
    return row_flux - backward_shift(row_flux, 1) + level_flux - backward_shift(level_flux, ROWS)


def zonal_weights(sea_float, sea_east, velocity):
    opened = sea_float * sea_east
    magnitude = jnp.abs(velocity)
    return jnp.stack(
        [
            opened * (-velocity - magnitude) / 12.0,
            opened * (7.0 * velocity + 3.0 * magnitude) / 12.0,
            opened * (7.0 * velocity - 3.0 * magnitude) / 12.0,
            opened * (magnitude - velocity) / 12.0,
        ]
    )


def trim_rim(source, keep_rim, outer_rim, dimension):
    length = source.shape[dimension] - 2 * outer_rim
    return lax.slice_in_dim(
        source, outer_rim - keep_rim, outer_rim + length + keep_rim, axis=dimension
    )


def surface_slopes(carbon, alkalinity, piston, surface_sea):

    def uptake_of(carbon_in, alkalinity_in):
        return chemistry(carbon_in, alkalinity_in, piston, surface_sea)

    uptake, pullback = jax.vjp(uptake_of, carbon, alkalinity)
    by_carbon, by_alkalinity = pullback(jnp.ones_like(carbon))
    return (uptake, jnp.stack([by_carbon, by_alkalinity]))


def advance_rim(extended, weights, row_weight, level_weight, uptake):
    length = extended.shape[1]
    face_flux = (
        weights[0, 1 : length - 2] * extended[:, 0 : length - 3]
        + weights[1, 1 : length - 2] * extended[:, 1 : length - 2]
        + weights[2, 1 : length - 2] * extended[:, 2 : length - 1]
        + weights[3, 1 : length - 2] * extended[:, 3:length]
    )
    interior = extended[:, 2 : length - 2]
    zonal_term = -(face_flux[:, 1:] - face_flux[:, :-1])
    transported = interior + zonal_term + column_mix(interior, row_weight, level_weight)
    surface_row = transported[0, :, :ROWS] + uptake
    carbon = jnp.concatenate([surface_row, transported[0, :, ROWS:]], axis=-1)
    return jnp.stack([carbon, transported[1]])


SPAN = 40
ORIGIN = 10


def halves(cells, axis, dim, width):
    count = lax.axis_size(axis)
    head = lax.slice_in_dim(cells, 0, width, axis=dim)
    tail = lax.slice_in_dim(cells, cells.shape[dim] - width, cells.shape[dim], axis=dim)
    west = lax.ppermute(tail, axis, [(i, (i + 1) % count) for i in range(count)])
    east = lax.ppermute(head, axis, [((i + 1) % count, i) for i in range(count)])
    return west, east


def placed_rows(source, first, total=SPAN):
    pad = [(0, 0)] * source.ndim
    pad[-2] = (first, total - first - source.shape[-2])
    return jnp.pad(source, pad)


def lanes_to(source, width):
    pad = [(0, 0)] * source.ndim
    pad[-1] = (0, width - source.shape[-1])
    return jnp.pad(source, pad)


def retreat_kernel(center_ref, west_ref, east_ref, w_ref, s_ref, seed_ref, out_ref, e_ref, f_ref):
    local = center_ref.shape[2]
    width = center_ref.shape[3]
    rim = west_ref.shape[2]
    e_ref[:, ORIGIN : ORIGIN + local, :] = center_ref[0]
    e_ref[:, ORIGIN - rim : ORIGIN, :] = west_ref[0]
    e_ref[:, ORIGIN + local : ORIGIN + local + rim, :] = east_ref[0]

    def block(src, r, t, stage):
        x_m2 = src[t, r - 2 : r + 6, :]
        x_m1 = src[t, r - 1 : r + 7, :]
        x_0 = src[t, r : r + 8, :]
        x_p1 = src[t, r + 1 : r + 9, :]
        x_p2 = src[t, r + 2 : r + 10, :]
        zonal = (
            w_ref[0, r : r + 8, :] * (x_p2 - x_p1)
            + w_ref[1, r : r + 8, :] * (x_p1 - x_0)
            + w_ref[2, r : r + 8, :] * (x_0 - x_m1)
            + w_ref[3, r : r + 8, :] * (x_m1 - x_m2)
        )
        row_flux = w_ref[4, r : r + 8, :] * (pltpu.roll(x_0, width - 1, 1) - x_0)
        level_flux = w_ref[5, r : r + 8, :] * (pltpu.roll(x_0, width - ROWS, 1) - x_0)
        mix = row_flux - pltpu.roll(row_flux, 1, 1) + level_flux - pltpu.roll(level_flux, ROWS, 1)
        adjoint = x_0 + zonal + mix
        forcing = src[0, r : r + 8, 0:128] + seed_ref[0, r : r + 8, :]
        head = adjoint[:, 0:128] + s_ref[stage, t, r : r + 8, :] * forcing
        return head, adjoint[:, 128:]

    for r in range(ORIGIN - 2, ORIGIN + local + 2, 8):
        for t in range(2):
            head, rest = block(e_ref, r, t, 0)
            f_ref[t, r : r + 8, 0:128] = head
            f_ref[t, r : r + 8, 128:] = rest
    for r in range(ORIGIN, ORIGIN + local, 8):
        for t in range(2):
            head, rest = block(f_ref, r, t, 1)
            out_ref[0, t, r - ORIGIN : r - ORIGIN + 8, 0:128] = head
            out_ref[0, t, r - ORIGIN : r - ORIGIN + 8, 128:] = rest


def two_retreats(center, west, east, stencil, slopes, seeds):
    groups, tracers, local, width = center.shape
    rim = west.shape[2]
    return pl.pallas_call(
        retreat_kernel,
        out_shape=jax.ShapeDtypeStruct(center.shape, center.dtype),
        grid=(groups,),
        in_specs=[
            pl.BlockSpec((1, tracers, local, width), lambda g: (g, 0, 0, 0)),
            pl.BlockSpec((1, tracers, rim, width), lambda g: (g, 0, 0, 0)),
            pl.BlockSpec((1, tracers, rim, width), lambda g: (g, 0, 0, 0)),
            pl.BlockSpec(stencil.shape, lambda g: (0, 0, 0)),
            pl.BlockSpec(slopes.shape, lambda g: (0, 0, 0, 0)),
            pl.BlockSpec((1,) + seeds.shape[1:], lambda g: (g, 0, 0)),
        ],
        out_specs=pl.BlockSpec((1, tracers, local, width), lambda g: (g, 0, 0, 0)),
        scratch_shapes=[
            pltpu.VMEM((tracers, SPAN, width), jnp.float32),
            pltpu.VMEM((tracers, SPAN, width), jnp.float32),
        ],
    )(center, west, east, stencil, slopes, seeds)


def staged(
    adjoint_in, checkpoint_store, interval, sea_mask, zonal_speed, mixing, piston, cell_area, region
):
    groups = adjoint_in.shape[0]
    cell_count = adjoint_in.shape[3]
    rim_depth = 4
    owners = lax.axis_size("obj")
    owner_index = interval[0] % owners
    band = 2 * ROWS
    stored = lax.dynamic_index_in_dim(checkpoint_store, interval[0] // owners, 0, keepdims=False)
    statics = jnp.concatenate(
        [
            stored[0, :, :band],
            stored[1, :, :band],
            sea_mask.astype(jnp.float32),
            zonal_speed,
            mixing,
            piston,
            cell_area,
            region.astype(jnp.float32),
        ],
        axis=1,
    )
    widened = padded(statics, (("tile", 0),), rim_depth)
    initial_wide = spread(
        jnp.stack([widened[:, :band], widened[:, band : 2 * band]]), "obj", owner_index
    )
    widened = widened[:, 2 * band :]
    sea_wide = widened[:, :cell_count]
    speed_wide = widened[:, cell_count : 2 * cell_count]
    mixing_wide = widened[:, 2 * cell_count : 3 * cell_count]
    offset = 3 * cell_count
    piston_wide = widened[:, offset : offset + ROWS]
    area_wide = widened[:, offset + ROWS : offset + 2 * ROWS]
    region_wide = widened[:, offset + 2 * ROWS : offset + 3 * ROWS]
    sea_east = jnp.concatenate([sea_wide[1:], jnp.zeros_like(sea_wide[:1])], axis=0)
    weights = zonal_weights(sea_wide, sea_east, speed_wide)
    row_weight, level_weight = column_weights(sea_wide, mixing_wide)
    surface_sea = sea_wide[:, :ROWS]
    targets = (lax.axis_index("obj") * groups + jnp.arange(groups, dtype=jnp.int32)).astype(
        jnp.float32
    )
    objective_seeds = area_wide[None] * (region_wide[None] == targets[:, None, None]).astype(
        jnp.float32
    )
    inner_rim = 2
    piston_inner = trim_rim(piston_wide, inner_rim, rim_depth, 0)
    sea_inner = trim_rim(surface_sea, inner_rim, rim_depth, 0)
    initial_inner = trim_rim(initial_wide, inner_rim, rim_depth, 1)
    uptake_first, slopes_first = surface_slopes(
        initial_inner[0, :, :ROWS], initial_inner[1, :, :ROWS], piston_inner, sea_inner
    )
    following = advance_rim(
        initial_wide,
        weights[:, :, :band],
        trim_rim(row_weight, inner_rim, rim_depth, 0)[:, :band],
        trim_rim(level_weight, inner_rim, rim_depth, 0)[:, :band],
        uptake_first,
    )
    _, slopes_second = surface_slopes(
        following[0, :, :ROWS], following[1, :, :ROWS], piston_inner, sea_inner
    )
    west, east = halves(adjoint_in, "tile", 2, rim_depth)
    first = ORIGIN - rim_depth
    stencil = jnp.stack(
        [
            placed_rows(weights[0], first - 1),
            placed_rows(weights[1], first),
            placed_rows(weights[2], first + 1),
            placed_rows(weights[3], first + 2),
            placed_rows(row_weight, first),
            placed_rows(level_weight, first),
        ]
    )
    slopes = lanes_to(
        jnp.stack(
            [
                placed_rows(slopes_second, ORIGIN - inner_rim),
                placed_rows(trim_rim(slopes_first, 0, inner_rim, 1), ORIGIN),
            ]
        ),
        128,
    )
    seeds = lanes_to(placed_rows(objective_seeds, first), 128)
    return two_retreats(adjoint_in, west, east, stencil, slopes, seeds)


def solution(mesh):
    placed = (
        P("obj", None, "tile", None),
        P("obj", None, "tile", None),
        P(),
        P("tile", None),
        P("tile", None),
        P("tile", None),
        P("tile", None),
        P("tile", None),
        P("tile", None),
    )
    return jax.shard_map(
        staged, mesh=mesh, in_specs=placed, out_specs=P("obj", None, "tile", None), check_vma=False
    )
```

```python
import jax
import jax.numpy as jnp
from jax import lax
from jax.sharding import PartitionSpec as P
from jax.experimental import pallas as pl
from jax.experimental.pallas import tpu as pltpu

ROWS = 32
LEVELS = 32
NEWTON = 4


DISSOCIATION_ONE = 1400.0
DISSOCIATION_TWO = 1.1
BORATE_CONSTANT = 2.5
BORON_TOTAL = 416.0
AIR_CARBON = 14.0
START_HYDROGEN = 2.0
ROW_DIFFUSION = 0.1


def padded(cells, sides, width):
    for axis, dim in sides:
        count = lax.axis_size(axis)
        head = lax.slice_in_dim(cells, 0, width, axis=dim)
        tail = lax.slice_in_dim(cells, cells.shape[dim] - width, cells.shape[dim], axis=dim)
        cells = jnp.concatenate(
            [
                lax.ppermute(tail, axis, [(i, (i + 1) % count) for i in range(count)]),
                cells,
                lax.ppermute(head, axis, [((i + 1) % count, i) for i in range(count)]),
            ],
            axis=dim,
        )
    return cells


def spread(value, axis, source):
    count = lax.axis_size(axis)
    top = count // 2
    if count < 2 or count & (count - 1):
        kept = jnp.where(lax.axis_index(axis) == source, value, 0).astype(value.dtype)
        return lax.psum(kept, axis)
    rank = jnp.bitwise_xor(lax.axis_index(axis), source)
    moved = lax.ppermute(value, axis, [(i, i ^ top) for i in range(count)])
    value = jnp.where(rank == top, moved, value)
    low = rank & (top - 1)
    received = value
    for mask in range(1, top):
        moved = lax.ppermute(value, axis, [(i, i ^ mask) for i in range(count)])
        received = jnp.where(low == mask, moved, received)
    return received


def chemistry(carbon, alkalinity, piston, surface_sea):
    hydrogen = jnp.full_like(carbon, START_HYDROGEN)
    for _ in range(NEWTON):
        square = hydrogen * hydrogen
        denominator = square + DISSOCIATION_ONE * hydrogen + DISSOCIATION_ONE * DISSOCIATION_TWO
        carbonate = carbon * DISSOCIATION_ONE * (hydrogen + 2.0 * DISSOCIATION_TWO) / denominator
        borate = BORON_TOTAL * BORATE_CONSTANT / (hydrogen + BORATE_CONSTANT)
        derivative = -carbon * DISSOCIATION_ONE * (
            square + 4.0 * DISSOCIATION_TWO * hydrogen + DISSOCIATION_ONE * DISSOCIATION_TWO
        ) / (denominator * denominator) - borate / (hydrogen + BORATE_CONSTANT)
        hydrogen = hydrogen - (carbonate + borate - alkalinity) / derivative
    square = hydrogen * hydrogen
    denominator = square + DISSOCIATION_ONE * hydrogen + DISSOCIATION_ONE * DISSOCIATION_TWO
    dissolved = carbon * square / denominator
    return surface_sea * piston * (AIR_CARBON - dissolved)


def forward_shift(source, offset):
    padding = jnp.zeros(source.shape[:-1] + (offset,), source.dtype)
    return jnp.concatenate([source[..., offset:], padding], axis=-1)


def backward_shift(source, offset):
    padding = jnp.zeros(source.shape[:-1] + (offset,), source.dtype)
    return jnp.concatenate([padding, source[..., :-offset]], axis=-1)


def column_weights(sea_float, mixing):
    cell_index = jnp.arange(LEVELS * ROWS, dtype=jnp.int32)
    row_open = (cell_index % ROWS < ROWS - 1).astype(jnp.float32)
    level_open = (cell_index // ROWS < LEVELS - 1).astype(jnp.float32)
    row_weight = ROW_DIFFUSION * row_open * sea_float * forward_shift(sea_float, 1)
    level_weight = mixing * level_open * sea_float * forward_shift(sea_float, ROWS)
    return (row_weight, level_weight)


def column_mix(source, row_weight, level_weight):
    row_flux = row_weight * (forward_shift(source, 1) - source)
    level_flux = level_weight * (forward_shift(source, ROWS) - source)
    return row_flux - backward_shift(row_flux, 1) + level_flux - backward_shift(level_flux, ROWS)


def zonal_weights(sea_float, sea_east, velocity):
    opened = sea_float * sea_east
    magnitude = jnp.abs(velocity)
    return jnp.stack(
        [
            opened * (-velocity - magnitude) / 12.0,
            opened * (7.0 * velocity + 3.0 * magnitude) / 12.0,
            opened * (7.0 * velocity - 3.0 * magnitude) / 12.0,
            opened * (magnitude - velocity) / 12.0,
        ]
    )


def trim_rim(source, keep_rim, outer_rim, dimension):
    length = source.shape[dimension] - 2 * outer_rim
    return lax.slice_in_dim(
        source, outer_rim - keep_rim, outer_rim + length + keep_rim, axis=dimension
    )


def surface_slopes(carbon, alkalinity, piston, surface_sea):

    def uptake_of(carbon_in, alkalinity_in):
        return chemistry(carbon_in, alkalinity_in, piston, surface_sea)

    uptake, pullback = jax.vjp(uptake_of, carbon, alkalinity)
    by_carbon, by_alkalinity = pullback(jnp.ones_like(carbon))
    return (uptake, jnp.stack([by_carbon, by_alkalinity]))


def advance_rim(extended, weights, row_weight, level_weight, uptake):
    length = extended.shape[1]
    face_flux = (
        weights[0, 1 : length - 2] * extended[:, 0 : length - 3]
        + weights[1, 1 : length - 2] * extended[:, 1 : length - 2]
        + weights[2, 1 : length - 2] * extended[:, 2 : length - 1]
        + weights[3, 1 : length - 2] * extended[:, 3:length]
    )
    interior = extended[:, 2 : length - 2]
    zonal_term = -(face_flux[:, 1:] - face_flux[:, :-1])
    transported = interior + zonal_term + column_mix(interior, row_weight, level_weight)
    surface_row = transported[0, :, :ROWS] + uptake
    carbon = jnp.concatenate([surface_row, transported[0, :, ROWS:]], axis=-1)
    return jnp.stack([carbon, transported[1]])


def halves(cells, axis, dim, width):
    count = lax.axis_size(axis)
    head = lax.slice_in_dim(cells, 0, width, axis=dim)
    tail = lax.slice_in_dim(cells, cells.shape[dim] - width, cells.shape[dim], axis=dim)
    west = lax.ppermute(tail, axis, [(i, (i + 1) % count) for i in range(count)])
    east = lax.ppermute(head, axis, [((i + 1) % count, i) for i in range(count)])
    return west, east


def cell_shift(x, step, lane, forward):
    if forward:
        turned = pltpu.roll(x, 128 - step, 1)
        carried = pltpu.roll(turned, 7, 0)
        return jnp.where(lane >= 128 - step, carried, turned)
    turned = pltpu.roll(x, step, 1)
    carried = pltpu.roll(turned, 1, 0)
    return jnp.where(lane < step, carried, turned)


def retreat_kernel(center_ref, west_ref, east_ref, w_ref, s_ref, seed_ref, out_ref, e_ref, f_ref):
    tracers = center_ref.shape[1]
    local = center_ref.shape[2]
    rim = west_ref.shape[2]
    lane = lax.broadcasted_iota(jnp.int32, (8, 128), 1)
    e_ref[:, rim : rim + local] = center_ref[0]
    e_ref[:, 0:rim] = west_ref[0]
    e_ref[:, rim + local : 2 * rim + local] = east_ref[0]

    def step(src, k, stage):
        w = [w_ref[m, k] for m in range(8)]
        results = []
        for t in range(tracers):
            x_0 = src[t, k]
            zonal = (
                w[0] * (src[t, k + 2] - src[t, k + 1])
                + w[1] * (src[t, k + 1] - x_0)
                + w[2] * (x_0 - src[t, k - 1])
                + w[3] * (src[t, k - 1] - src[t, k - 2])
            )
            mix = (
                w[4] * (cell_shift(x_0, 1, lane, True) - x_0)
                - w[5] * (x_0 - cell_shift(x_0, 1, lane, False))
                + w[6] * (cell_shift(x_0, ROWS, lane, True) - x_0)
                - w[7] * (x_0 - cell_shift(x_0, ROWS, lane, False))
            )
            forcing = src[0, k] + seed_ref[0, k]
            results.append(x_0 + zonal + mix + s_ref[stage, t, k] * forcing)
        return results

    def first(k, carry):
        for t, value in enumerate(step(e_ref, k, 0)):
            f_ref[t, k] = value
        return carry

    def second(k, carry):
        for t, value in enumerate(step(f_ref, k, 1)):
            out_ref[0, t, k - rim] = value
        return carry

    lax.fori_loop(2, 2 * rim + local - 2, first, 0, unroll=True)
    lax.fori_loop(rim, rim + local, second, 0, unroll=True)


def two_retreats(center, west, east, stencil, slopes, seeds):
    groups, tracers, local, sub, lanes = center.shape
    rim = west.shape[2]
    span = local + 2 * rim
    return pl.pallas_call(
        retreat_kernel,
        out_shape=jax.ShapeDtypeStruct(center.shape, center.dtype),
        grid=(groups,),
        in_specs=[
            pl.BlockSpec((1, tracers, local, sub, lanes), lambda g: (g, 0, 0, 0, 0)),
            pl.BlockSpec((1, tracers, rim, sub, lanes), lambda g: (g, 0, 0, 0, 0)),
            pl.BlockSpec((1, tracers, rim, sub, lanes), lambda g: (g, 0, 0, 0, 0)),
            pl.BlockSpec(stencil.shape, lambda g: (0, 0, 0, 0)),
            pl.BlockSpec(slopes.shape, lambda g: (0, 0, 0, 0, 0)),
            pl.BlockSpec((1,) + seeds.shape[1:], lambda g: (g, 0, 0, 0)),
        ],
        out_specs=pl.BlockSpec((1, tracers, local, sub, lanes), lambda g: (g, 0, 0, 0, 0)),
        scratch_shapes=[
            pltpu.VMEM((tracers, span, sub, lanes), jnp.float32),
            pltpu.VMEM((tracers, span, sub, lanes), jnp.float32),
        ],
    )(center, west, east, stencil, slopes, seeds)


def as_tiles(source):
    return source.reshape(source.shape[:-1] + (source.shape[-1] // 128, 128))


def staged(
    adjoint_in, checkpoint_store, interval, sea_mask, zonal_speed, mixing, piston, cell_area, region
):
    groups = adjoint_in.shape[0]
    cell_count = adjoint_in.shape[3]
    rim_depth = 4
    owners = lax.axis_size("obj")
    owner_index = interval[0] % owners
    band = 2 * ROWS
    stored = lax.dynamic_index_in_dim(checkpoint_store, interval[0] // owners, 0, keepdims=False)
    statics = jnp.concatenate(
        [
            stored[0, :, :band],
            stored[1, :, :band],
            sea_mask.astype(jnp.float32),
            zonal_speed,
            mixing,
            piston,
            cell_area,
            region.astype(jnp.float32),
        ],
        axis=1,
    )
    widened = padded(statics, (("tile", 0),), rim_depth)
    initial_wide = spread(
        jnp.stack([widened[:, :band], widened[:, band : 2 * band]]), "obj", owner_index
    )
    widened = widened[:, 2 * band :]
    sea_wide = widened[:, :cell_count]
    speed_wide = widened[:, cell_count : 2 * cell_count]
    mixing_wide = widened[:, 2 * cell_count : 3 * cell_count]
    offset = 3 * cell_count
    piston_wide = widened[:, offset : offset + ROWS]
    area_wide = widened[:, offset + ROWS : offset + 2 * ROWS]
    region_wide = widened[:, offset + 2 * ROWS : offset + 3 * ROWS]
    sea_east = jnp.concatenate([sea_wide[1:], jnp.zeros_like(sea_wide[:1])], axis=0)
    weights = zonal_weights(sea_wide, sea_east, speed_wide)
    row_weight, level_weight = column_weights(sea_wide, mixing_wide)
    surface_sea = sea_wide[:, :ROWS]
    targets = (lax.axis_index("obj") * groups + jnp.arange(groups, dtype=jnp.int32)).astype(
        jnp.float32
    )
    objective_seeds = area_wide[None] * (region_wide[None] == targets[:, None, None]).astype(
        jnp.float32
    )
    inner_rim = 2
    piston_inner = trim_rim(piston_wide, inner_rim, rim_depth, 0)
    sea_inner = trim_rim(surface_sea, inner_rim, rim_depth, 0)
    initial_inner = trim_rim(initial_wide, inner_rim, rim_depth, 1)
    uptake_first, slopes_first = surface_slopes(
        initial_inner[0, :, :ROWS], initial_inner[1, :, :ROWS], piston_inner, sea_inner
    )
    following = advance_rim(
        initial_wide,
        weights[:, :, :band],
        trim_rim(row_weight, inner_rim, rim_depth, 0)[:, :band],
        trim_rim(level_weight, inner_rim, rim_depth, 0)[:, :band],
        uptake_first,
    )
    _, slopes_second = surface_slopes(
        following[0, :, :ROWS], following[1, :, :ROWS], piston_inner, sea_inner
    )
    west, east = halves(as_tiles(adjoint_in), "tile", 2, rim_depth)
    span = adjoint_in.shape[2] + 2 * rim_depth

    def along(source, lead):
        pad = [(0, 0)] * source.ndim
        pad[0] = (lead, span - lead - source.shape[0])
        return jnp.pad(source, pad)

    def cells_of(source):
        pad = [(0, 0)] * source.ndim
        pad[-1] = (0, cell_count - source.shape[-1])
        return jnp.pad(source, pad)

    wide = weights.shape[1]
    stencil = as_tiles(
        jnp.stack(
            [
                along(weights[0][1:], 0),
                weights[1],
                along(weights[2][: wide - 1], 1),
                along(weights[3][: wide - 2], 2),
                row_weight,
                backward_shift(row_weight, 1),
                level_weight,
                backward_shift(level_weight, ROWS),
            ]
        )
    )
    second = jnp.moveaxis(slopes_second, 1, 0)
    first_slopes = jnp.moveaxis(trim_rim(slopes_first, 0, inner_rim, 1), 1, 0)
    slopes = as_tiles(
        cells_of(
            jnp.stack(
                [
                    jnp.moveaxis(along(second, inner_rim), 0, 1),
                    jnp.moveaxis(along(first_slopes, rim_depth), 0, 1),
                ]
            )
        )
    )
    seeds = as_tiles(cells_of(objective_seeds))
    out = two_retreats(as_tiles(adjoint_in), west, east, stencil, slopes, seeds)
    return out.reshape(adjoint_in.shape)


def solution(mesh):
    placed = (
        P("obj", None, "tile", None),
        P("obj", None, "tile", None),
        P(),
        P("tile", None),
        P("tile", None),
        P("tile", None),
        P("tile", None),
        P("tile", None),
        P("tile", None),
    )
    return jax.shard_map(
        staged, mesh=mesh, in_specs=placed, out_specs=P("obj", None, "tile", None), check_vma=False
    )
```

```python
import jax
import jax.numpy as jnp
from jax import lax
from jax.sharding import PartitionSpec as P
from jax.experimental import pallas as pl
from jax.experimental.pallas import tpu as pltpu

ROWS = 32
LEVELS = 32
NEWTON = 4


DISSOCIATION_ONE = 1400.0
DISSOCIATION_TWO = 1.1
BORATE_CONSTANT = 2.5
BORON_TOTAL = 416.0
AIR_CARBON = 14.0
START_HYDROGEN = 2.0
ROW_DIFFUSION = 0.1


def padded(cells, sides, width):
    for axis, dim in sides:
        count = lax.axis_size(axis)
        head = lax.slice_in_dim(cells, 0, width, axis=dim)
        tail = lax.slice_in_dim(cells, cells.shape[dim] - width, cells.shape[dim], axis=dim)
        cells = jnp.concatenate(
            [
                lax.ppermute(tail, axis, [(i, (i + 1) % count) for i in range(count)]),
                cells,
                lax.ppermute(head, axis, [((i + 1) % count, i) for i in range(count)]),
            ],
            axis=dim,
        )
    return cells


def spread(value, axis, source):
    count = lax.axis_size(axis)
    top = count // 2
    if count < 2 or count & (count - 1):
        kept = jnp.where(lax.axis_index(axis) == source, value, 0).astype(value.dtype)
        return lax.psum(kept, axis)
    rank = jnp.bitwise_xor(lax.axis_index(axis), source)
    moved = lax.ppermute(value, axis, [(i, i ^ top) for i in range(count)])
    value = jnp.where(rank == top, moved, value)
    low = rank & (top - 1)
    received = value
    for mask in range(1, top):
        moved = lax.ppermute(value, axis, [(i, i ^ mask) for i in range(count)])
        received = jnp.where(low == mask, moved, received)
    return received


def chemistry(carbon, alkalinity, piston, surface_sea):
    hydrogen = jnp.full_like(carbon, START_HYDROGEN)
    for _ in range(NEWTON):
        square = hydrogen * hydrogen
        denominator = square + DISSOCIATION_ONE * hydrogen + DISSOCIATION_ONE * DISSOCIATION_TWO
        carbonate = carbon * DISSOCIATION_ONE * (hydrogen + 2.0 * DISSOCIATION_TWO) / denominator
        borate = BORON_TOTAL * BORATE_CONSTANT / (hydrogen + BORATE_CONSTANT)
        derivative = -carbon * DISSOCIATION_ONE * (
            square + 4.0 * DISSOCIATION_TWO * hydrogen + DISSOCIATION_ONE * DISSOCIATION_TWO
        ) / (denominator * denominator) - borate / (hydrogen + BORATE_CONSTANT)
        hydrogen = hydrogen - (carbonate + borate - alkalinity) / derivative
    square = hydrogen * hydrogen
    denominator = square + DISSOCIATION_ONE * hydrogen + DISSOCIATION_ONE * DISSOCIATION_TWO
    dissolved = carbon * square / denominator
    return surface_sea * piston * (AIR_CARBON - dissolved)


def forward_shift(source, offset):
    padding = jnp.zeros(source.shape[:-1] + (offset,), source.dtype)
    return jnp.concatenate([source[..., offset:], padding], axis=-1)


def backward_shift(source, offset):
    padding = jnp.zeros(source.shape[:-1] + (offset,), source.dtype)
    return jnp.concatenate([padding, source[..., :-offset]], axis=-1)


def column_weights(sea_float, mixing):
    cell_index = jnp.arange(LEVELS * ROWS, dtype=jnp.int32)
    row_open = (cell_index % ROWS < ROWS - 1).astype(jnp.float32)
    level_open = (cell_index // ROWS < LEVELS - 1).astype(jnp.float32)
    row_weight = ROW_DIFFUSION * row_open * sea_float * forward_shift(sea_float, 1)
    level_weight = mixing * level_open * sea_float * forward_shift(sea_float, ROWS)
    return (row_weight, level_weight)


def column_mix(source, row_weight, level_weight):
    row_flux = row_weight * (forward_shift(source, 1) - source)
    level_flux = level_weight * (forward_shift(source, ROWS) - source)
    return row_flux - backward_shift(row_flux, 1) + level_flux - backward_shift(level_flux, ROWS)


def zonal_weights(sea_float, sea_east, velocity):
    opened = sea_float * sea_east
    magnitude = jnp.abs(velocity)
    return jnp.stack(
        [
            opened * (-velocity - magnitude) / 12.0,
            opened * (7.0 * velocity + 3.0 * magnitude) / 12.0,
            opened * (7.0 * velocity - 3.0 * magnitude) / 12.0,
            opened * (magnitude - velocity) / 12.0,
        ]
    )


def trim_rim(source, keep_rim, outer_rim, dimension):
    length = source.shape[dimension] - 2 * outer_rim
    return lax.slice_in_dim(
        source, outer_rim - keep_rim, outer_rim + length + keep_rim, axis=dimension
    )


def surface_slopes(carbon, alkalinity, piston, surface_sea):

    def uptake_of(carbon_in, alkalinity_in):
        return chemistry(carbon_in, alkalinity_in, piston, surface_sea)

    uptake, pullback = jax.vjp(uptake_of, carbon, alkalinity)
    by_carbon, by_alkalinity = pullback(jnp.ones_like(carbon))
    return (uptake, jnp.stack([by_carbon, by_alkalinity]))


def advance_rim(extended, weights, row_weight, level_weight, uptake):
    length = extended.shape[1]
    face_flux = (
        weights[0, 1 : length - 2] * extended[:, 0 : length - 3]
        + weights[1, 1 : length - 2] * extended[:, 1 : length - 2]
        + weights[2, 1 : length - 2] * extended[:, 2 : length - 1]
        + weights[3, 1 : length - 2] * extended[:, 3:length]
    )
    interior = extended[:, 2 : length - 2]
    zonal_term = -(face_flux[:, 1:] - face_flux[:, :-1])
    transported = interior + zonal_term + column_mix(interior, row_weight, level_weight)
    surface_row = transported[0, :, :ROWS] + uptake
    carbon = jnp.concatenate([surface_row, transported[0, :, ROWS:]], axis=-1)
    return jnp.stack([carbon, transported[1]])


def halves(cells, axis, dim, width):
    count = lax.axis_size(axis)
    head = lax.slice_in_dim(cells, 0, width, axis=dim)
    tail = lax.slice_in_dim(cells, cells.shape[dim] - width, cells.shape[dim], axis=dim)
    west = lax.ppermute(tail, axis, [(i, (i + 1) % count) for i in range(count)])
    east = lax.ppermute(head, axis, [((i + 1) % count, i) for i in range(count)])
    return west, east


def cell_shift(x, step, lane, forward):
    if forward:
        turned = pltpu.roll(x, 128 - step, 1)
        carried = pltpu.roll(turned, 7, 0)
        return jnp.where(lane >= 128 - step, carried, turned)
    turned = pltpu.roll(x, step, 1)
    carried = pltpu.roll(turned, 1, 0)
    return jnp.where(lane < step, carried, turned)


def stencil_step(src, k, stage, shift, w_ref, s_ref, seed_ref, lane):
    w = [w_ref[m, k + shift] for m in range(8)]
    results = []
    for t in range(src.shape[0]):
        x_0 = src[t, k]
        zonal = (
            w[0] * (src[t, k + 2] - src[t, k + 1])
            + w[1] * (src[t, k + 1] - x_0)
            + w[2] * (x_0 - src[t, k - 1])
            + w[3] * (src[t, k - 1] - src[t, k - 2])
        )
        mix = (
            w[4] * (cell_shift(x_0, 1, lane, True) - x_0)
            - w[5] * (x_0 - cell_shift(x_0, 1, lane, False))
            + w[6] * (cell_shift(x_0, ROWS, lane, True) - x_0)
            - w[7] * (x_0 - cell_shift(x_0, ROWS, lane, False))
        )
        forcing = src[0, k] + seed_ref[0, k + shift]
        results.append(x_0 + zonal + mix + s_ref[stage, t, k + shift] * forcing)
    return results


def run_steps(e_ref, f_ref, out_ref, first_rows, second_rows, shift, out_start, refs):
    w_ref, s_ref, seed_ref = refs
    lane = lax.broadcasted_iota(jnp.int32, (8, 128), 1)
    for k in first_rows:
        for t, value in enumerate(stencil_step(e_ref, k, 0, shift, w_ref, s_ref, seed_ref, lane)):
            f_ref[t, k] = value
    for k in second_rows:
        for t, value in enumerate(stencil_step(f_ref, k, 1, shift, w_ref, s_ref, seed_ref, lane)):
            out_ref[0, t, k - out_start] = value


def interior_kernel(center_ref, w_ref, s_ref, seed_ref, out_ref, e_ref, f_ref):
    local = center_ref.shape[2]
    rim = (w_ref.shape[1] - local) // 2
    e_ref[...] = center_ref[0]
    run_steps(
        e_ref, f_ref, out_ref, range(2, local - 2), range(rim, local - rim), rim, 0,
        (w_ref, s_ref, seed_ref),
    )


def edge_kernel(center_ref, west_ref, east_ref, w_ref, s_ref, seed_ref, done_ref, out_ref, e_ref, f_ref):
    del done_ref
    local = center_ref.shape[2]
    rim = west_ref.shape[2]
    side = pl.program_id(1)

    @pl.when(side == 0)
    def _():
        e_ref[:, 0:rim] = west_ref[0]
        e_ref[:, rim : 3 * rim] = center_ref[0, :, 0 : 2 * rim]
        run_steps(
            e_ref, f_ref, out_ref, range(2, 3 * rim - 2), range(rim, 2 * rim), 0, rim,
            (w_ref, s_ref, seed_ref),
        )

    @pl.when(side == 1)
    def _():
        e_ref[:, 0 : 2 * rim] = center_ref[0, :, local - 2 * rim : local]
        e_ref[:, 2 * rim : 3 * rim] = east_ref[0]
        run_steps(
            e_ref, f_ref, out_ref, range(2, 3 * rim - 2), range(rim, 2 * rim), local - rim, rim,
            (w_ref, s_ref, seed_ref),
        )


def two_retreats(center, west, east, stencil, slopes, seeds):
    groups, tracers, local, sub, lanes = center.shape
    rim = west.shape[2]
    tile = (sub, lanes)
    whole = (1, tracers, local) + tile
    shared = [
        pl.BlockSpec(stencil.shape, lambda *g: (0, 0, 0, 0)),
        pl.BlockSpec(slopes.shape, lambda *g: (0, 0, 0, 0, 0)),
        pl.BlockSpec((1,) + seeds.shape[1:], lambda g, *e: (g, 0, 0, 0)),
    ]
    inner = pl.pallas_call(
        interior_kernel,
        out_shape=jax.ShapeDtypeStruct(center.shape, center.dtype),
        grid=(groups,),
        in_specs=[pl.BlockSpec(whole, lambda g: (g, 0, 0, 0, 0))] + shared,
        out_specs=pl.BlockSpec(whole, lambda g: (g, 0, 0, 0, 0)),
        scratch_shapes=[
            pltpu.VMEM((tracers, local) + tile, jnp.float32),
            pltpu.VMEM((tracers, local) + tile, jnp.float32),
        ],
    )(center, stencil, slopes, seeds)
    edge = (1, tracers, rim) + tile
    last = local // rim - 1
    return pl.pallas_call(
        edge_kernel,
        out_shape=jax.ShapeDtypeStruct(center.shape, center.dtype),
        grid=(groups, 2),
        in_specs=[
            pl.BlockSpec(whole, lambda g, e: (g, 0, 0, 0, 0)),
            pl.BlockSpec(edge, lambda g, e: (g, 0, 0, 0, 0)),
            pl.BlockSpec(edge, lambda g, e: (g, 0, 0, 0, 0)),
        ]
        + shared
        + [pl.BlockSpec(memory_space=pl.ANY)],
        out_specs=pl.BlockSpec(edge, lambda g, e: (g, 0, e * last, 0, 0)),
        scratch_shapes=[
            pltpu.VMEM((tracers, 3 * rim) + tile, jnp.float32),
            pltpu.VMEM((tracers, 3 * rim) + tile, jnp.float32),
        ],
        input_output_aliases={6: 0},
    )(center, west, east, stencil, slopes, seeds, inner)


def as_tiles(source):
    return source.reshape(source.shape[:-1] + (source.shape[-1] // 128, 128))


def staged(
    adjoint_in, checkpoint_store, interval, sea_mask, zonal_speed, mixing, piston, cell_area, region
):
    groups = adjoint_in.shape[0]
    cell_count = adjoint_in.shape[3]
    rim_depth = 4
    owners = lax.axis_size("obj")
    owner_index = interval[0] % owners
    band = 2 * ROWS
    stored = lax.dynamic_index_in_dim(checkpoint_store, interval[0] // owners, 0, keepdims=False)
    statics = jnp.concatenate(
        [
            stored[0, :, :band],
            stored[1, :, :band],
            sea_mask.astype(jnp.float32),
            zonal_speed,
            mixing,
            piston,
            cell_area,
            region.astype(jnp.float32),
        ],
        axis=1,
    )
    widened = padded(statics, (("tile", 0),), rim_depth)
    initial_wide = spread(
        jnp.stack([widened[:, :band], widened[:, band : 2 * band]]), "obj", owner_index
    )
    widened = widened[:, 2 * band :]
    sea_wide = widened[:, :cell_count]
    speed_wide = widened[:, cell_count : 2 * cell_count]
    mixing_wide = widened[:, 2 * cell_count : 3 * cell_count]
    offset = 3 * cell_count
    piston_wide = widened[:, offset : offset + ROWS]
    area_wide = widened[:, offset + ROWS : offset + 2 * ROWS]
    region_wide = widened[:, offset + 2 * ROWS : offset + 3 * ROWS]
    sea_east = jnp.concatenate([sea_wide[1:], jnp.zeros_like(sea_wide[:1])], axis=0)
    weights = zonal_weights(sea_wide, sea_east, speed_wide)
    row_weight, level_weight = column_weights(sea_wide, mixing_wide)
    surface_sea = sea_wide[:, :ROWS]
    targets = (lax.axis_index("obj") * groups + jnp.arange(groups, dtype=jnp.int32)).astype(
        jnp.float32
    )
    objective_seeds = area_wide[None] * (region_wide[None] == targets[:, None, None]).astype(
        jnp.float32
    )
    inner_rim = 2
    piston_inner = trim_rim(piston_wide, inner_rim, rim_depth, 0)
    sea_inner = trim_rim(surface_sea, inner_rim, rim_depth, 0)
    initial_inner = trim_rim(initial_wide, inner_rim, rim_depth, 1)
    uptake_first, slopes_first = surface_slopes(
        initial_inner[0, :, :ROWS], initial_inner[1, :, :ROWS], piston_inner, sea_inner
    )
    following = advance_rim(
        initial_wide,
        weights[:, :, :band],
        trim_rim(row_weight, inner_rim, rim_depth, 0)[:, :band],
        trim_rim(level_weight, inner_rim, rim_depth, 0)[:, :band],
        uptake_first,
    )
    _, slopes_second = surface_slopes(
        following[0, :, :ROWS], following[1, :, :ROWS], piston_inner, sea_inner
    )
    west, east = halves(as_tiles(adjoint_in), "tile", 2, rim_depth)
    span = adjoint_in.shape[2] + 2 * rim_depth

    def along(source, lead):
        pad = [(0, 0)] * source.ndim
        pad[0] = (lead, span - lead - source.shape[0])
        return jnp.pad(source, pad)

    def cells_of(source):
        pad = [(0, 0)] * source.ndim
        pad[-1] = (0, cell_count - source.shape[-1])
        return jnp.pad(source, pad)

    wide = weights.shape[1]
    stencil = as_tiles(
        jnp.stack(
            [
                along(weights[0][1:], 0),
                weights[1],
                along(weights[2][: wide - 1], 1),
                along(weights[3][: wide - 2], 2),
                row_weight,
                backward_shift(row_weight, 1),
                level_weight,
                backward_shift(level_weight, ROWS),
            ]
        )
    )
    second = jnp.moveaxis(slopes_second, 1, 0)
    first_slopes = jnp.moveaxis(trim_rim(slopes_first, 0, inner_rim, 1), 1, 0)
    slopes = as_tiles(
        cells_of(
            jnp.stack(
                [
                    jnp.moveaxis(along(second, inner_rim), 0, 1),
                    jnp.moveaxis(along(first_slopes, rim_depth), 0, 1),
                ]
            )
        )
    )
    seeds = as_tiles(cells_of(objective_seeds))
    out = two_retreats(as_tiles(adjoint_in), west, east, stencil, slopes, seeds)
    return out.reshape(adjoint_in.shape)


def solution(mesh):
    placed = (
        P("obj", None, "tile", None),
        P("obj", None, "tile", None),
        P(),
        P("tile", None),
        P("tile", None),
        P("tile", None),
        P("tile", None),
        P("tile", None),
        P("tile", None),
    )
    return jax.shard_map(
        staged, mesh=mesh, in_specs=placed, out_specs=P("obj", None, "tile", None), check_vma=False
    )
```

```python
import jax
import jax.numpy as jnp
from jax import lax
from jax.sharding import PartitionSpec as P
from jax.experimental import pallas as pl
from jax.experimental.pallas import tpu as pltpu

ROWS = 32
LEVELS = 32
NEWTON = 4


DISSOCIATION_ONE = 1400.0
DISSOCIATION_TWO = 1.1
BORATE_CONSTANT = 2.5
BORON_TOTAL = 416.0
AIR_CARBON = 14.0
START_HYDROGEN = 2.0
ROW_DIFFUSION = 0.1


def padded(cells, sides, width):
    for axis, dim in sides:
        count = lax.axis_size(axis)
        head = lax.slice_in_dim(cells, 0, width, axis=dim)
        tail = lax.slice_in_dim(cells, cells.shape[dim] - width, cells.shape[dim], axis=dim)
        cells = jnp.concatenate(
            [
                lax.ppermute(tail, axis, [(i, (i + 1) % count) for i in range(count)]),
                cells,
                lax.ppermute(head, axis, [((i + 1) % count, i) for i in range(count)]),
            ],
            axis=dim,
        )
    return cells


def spread(value, axis, source):
    count = lax.axis_size(axis)
    top = count // 2
    if count < 2 or count & (count - 1):
        kept = jnp.where(lax.axis_index(axis) == source, value, 0).astype(value.dtype)
        return lax.psum(kept, axis)
    rank = jnp.bitwise_xor(lax.axis_index(axis), source)
    moved = lax.ppermute(value, axis, [(i, i ^ top) for i in range(count)])
    value = jnp.where(rank == top, moved, value)
    low = rank & (top - 1)
    received = value
    for mask in range(1, top):
        moved = lax.ppermute(value, axis, [(i, i ^ mask) for i in range(count)])
        received = jnp.where(low == mask, moved, received)
    return received


def chemistry(carbon, alkalinity, piston, surface_sea):
    hydrogen = jnp.full_like(carbon, START_HYDROGEN)
    for _ in range(NEWTON):
        square = hydrogen * hydrogen
        denominator = square + DISSOCIATION_ONE * hydrogen + DISSOCIATION_ONE * DISSOCIATION_TWO
        carbonate = carbon * DISSOCIATION_ONE * (hydrogen + 2.0 * DISSOCIATION_TWO) / denominator
        borate = BORON_TOTAL * BORATE_CONSTANT / (hydrogen + BORATE_CONSTANT)
        derivative = -carbon * DISSOCIATION_ONE * (
            square + 4.0 * DISSOCIATION_TWO * hydrogen + DISSOCIATION_ONE * DISSOCIATION_TWO
        ) / (denominator * denominator) - borate / (hydrogen + BORATE_CONSTANT)
        hydrogen = hydrogen - (carbonate + borate - alkalinity) / derivative
    square = hydrogen * hydrogen
    denominator = square + DISSOCIATION_ONE * hydrogen + DISSOCIATION_ONE * DISSOCIATION_TWO
    dissolved = carbon * square / denominator
    return surface_sea * piston * (AIR_CARBON - dissolved)


def forward_shift(source, offset):
    padding = jnp.zeros(source.shape[:-1] + (offset,), source.dtype)
    return jnp.concatenate([source[..., offset:], padding], axis=-1)


def backward_shift(source, offset):
    padding = jnp.zeros(source.shape[:-1] + (offset,), source.dtype)
    return jnp.concatenate([padding, source[..., :-offset]], axis=-1)


def column_weights(sea_float, mixing):
    cell_index = jnp.arange(LEVELS * ROWS, dtype=jnp.int32)
    row_open = (cell_index % ROWS < ROWS - 1).astype(jnp.float32)
    level_open = (cell_index // ROWS < LEVELS - 1).astype(jnp.float32)
    row_weight = ROW_DIFFUSION * row_open * sea_float * forward_shift(sea_float, 1)
    level_weight = mixing * level_open * sea_float * forward_shift(sea_float, ROWS)
    return (row_weight, level_weight)


def column_mix(source, row_weight, level_weight):
    row_flux = row_weight * (forward_shift(source, 1) - source)
    level_flux = level_weight * (forward_shift(source, ROWS) - source)
    return row_flux - backward_shift(row_flux, 1) + level_flux - backward_shift(level_flux, ROWS)


def zonal_weights(sea_float, sea_east, velocity):
    opened = sea_float * sea_east
    magnitude = jnp.abs(velocity)
    return jnp.stack(
        [
            opened * (-velocity - magnitude) / 12.0,
            opened * (7.0 * velocity + 3.0 * magnitude) / 12.0,
            opened * (7.0 * velocity - 3.0 * magnitude) / 12.0,
            opened * (magnitude - velocity) / 12.0,
        ]
    )


def trim_rim(source, keep_rim, outer_rim, dimension):
    length = source.shape[dimension] - 2 * outer_rim
    return lax.slice_in_dim(
        source, outer_rim - keep_rim, outer_rim + length + keep_rim, axis=dimension
    )


def surface_slopes(carbon, alkalinity, piston, surface_sea):

    def uptake_of(carbon_in, alkalinity_in):
        return chemistry(carbon_in, alkalinity_in, piston, surface_sea)

    uptake, pullback = jax.vjp(uptake_of, carbon, alkalinity)
    by_carbon, by_alkalinity = pullback(jnp.ones_like(carbon))
    return (uptake, jnp.stack([by_carbon, by_alkalinity]))


def advance_rim(extended, weights, row_weight, level_weight, uptake):
    length = extended.shape[1]
    face_flux = (
        weights[0, 1 : length - 2] * extended[:, 0 : length - 3]
        + weights[1, 1 : length - 2] * extended[:, 1 : length - 2]
        + weights[2, 1 : length - 2] * extended[:, 2 : length - 1]
        + weights[3, 1 : length - 2] * extended[:, 3:length]
    )
    interior = extended[:, 2 : length - 2]
    zonal_term = -(face_flux[:, 1:] - face_flux[:, :-1])
    transported = interior + zonal_term + column_mix(interior, row_weight, level_weight)
    surface_row = transported[0, :, :ROWS] + uptake
    carbon = jnp.concatenate([surface_row, transported[0, :, ROWS:]], axis=-1)
    return jnp.stack([carbon, transported[1]])


def halves(cells, axis, dim, width):
    count = lax.axis_size(axis)
    head = lax.slice_in_dim(cells, 0, width, axis=dim)
    tail = lax.slice_in_dim(cells, cells.shape[dim] - width, cells.shape[dim], axis=dim)
    west = lax.ppermute(tail, axis, [(i, (i + 1) % count) for i in range(count)])
    east = lax.ppermute(head, axis, [((i + 1) % count, i) for i in range(count)])
    return west, east


def lanes_to(source, width):
    pad = [(0, 0)] * source.ndim
    pad[-1] = (0, width - source.shape[-1])
    return jnp.pad(source, pad)


def cell_shift(x, step, lane, forward):
    if forward:
        turned = pltpu.roll(x, 128 - step, 1)
        carried = pltpu.roll(turned, 7, 0)
        return jnp.where(lane >= 128 - step, carried, turned)
    turned = pltpu.roll(x, step, 1)
    carried = pltpu.roll(turned, 1, 0)
    return jnp.where(lane < step, carried, turned)


def retreat_kernel(center_ref, west_ref, east_ref, w_ref, s_ref, seed_ref, out_ref, e_ref, f_ref):
    tracers = center_ref.shape[1]
    local = center_ref.shape[2]
    rim = west_ref.shape[2]
    lane = lax.broadcasted_iota(jnp.int32, (8, 128), 1)
    e_ref[:, rim : rim + local] = center_ref[0]
    e_ref[:, 0:rim] = west_ref[0]
    e_ref[:, rim + local : 2 * rim + local] = east_ref[0]

    def step(src, k, stage):
        w = [w_ref[m, k] for m in range(8)]
        results = []
        for t in range(tracers):
            x_0 = src[t, k]
            zonal = (
                w[0] * (src[t, k + 2] - src[t, k + 1])
                + w[1] * (src[t, k + 1] - x_0)
                + w[2] * (x_0 - src[t, k - 1])
                + w[3] * (src[t, k - 1] - src[t, k - 2])
            )
            mix = (
                w[4] * (cell_shift(x_0, 1, lane, True) - x_0)
                - w[5] * (x_0 - cell_shift(x_0, 1, lane, False))
                + w[6] * (cell_shift(x_0, ROWS, lane, True) - x_0)
                - w[7] * (x_0 - cell_shift(x_0, ROWS, lane, False))
            )
            forcing = src[0, k] + seed_ref[0, k]
            results.append(x_0 + zonal + mix + s_ref[stage, t, k] * forcing)
        return results

    def first(k, carry):
        for t, value in enumerate(step(e_ref, k, 0)):
            f_ref[t, k] = value
        return carry

    def second(k, carry):
        for t, value in enumerate(step(f_ref, k, 1)):
            out_ref[0, t, k - rim] = value
        return carry

    lax.fori_loop(2, 2 * rim + local - 2, first, 0, unroll=True)
    lax.fori_loop(rim, rim + local, second, 0, unroll=True)


def two_retreats(center, west, east, stencil, slopes, seeds):
    groups, tracers, local, sub, lanes = center.shape
    rim = west.shape[2]
    span = local + 2 * rim
    return pl.pallas_call(
        retreat_kernel,
        out_shape=jax.ShapeDtypeStruct(center.shape, center.dtype),
        grid=(groups,),
        in_specs=[
            pl.BlockSpec((1, tracers, local, sub, lanes), lambda g: (g, 0, 0, 0, 0)),
            pl.BlockSpec((1, tracers, rim, sub, lanes), lambda g: (g, 0, 0, 0, 0)),
            pl.BlockSpec((1, tracers, rim, sub, lanes), lambda g: (g, 0, 0, 0, 0)),
            pl.BlockSpec(stencil.shape, lambda g: (0, 0, 0, 0)),
            pl.BlockSpec(slopes.shape, lambda g: (0, 0, 0, 0, 0)),
            pl.BlockSpec((1,) + seeds.shape[1:], lambda g: (g, 0, 0, 0)),
        ],
        out_specs=pl.BlockSpec((1, tracers, local, sub, lanes), lambda g: (g, 0, 0, 0, 0)),
        scratch_shapes=[
            pltpu.VMEM((tracers, span, sub, lanes), jnp.float32),
            pltpu.VMEM((tracers, span, sub, lanes), jnp.float32),
        ],
    )(center, west, east, stencil, slopes, seeds)


def as_tiles(source):
    return source.reshape(source.shape[:-1] + (source.shape[-1] // 128, 128))


def staged(
    adjoint_in, checkpoint_store, interval, sea_mask, zonal_speed, mixing, piston, cell_area, region
):
    groups = adjoint_in.shape[0]
    cell_count = adjoint_in.shape[3]
    rim_depth = 4
    owners = lax.axis_size("obj")
    owner_index = interval[0] % owners
    band = 2 * ROWS
    stored = lax.dynamic_index_in_dim(checkpoint_store, interval[0] // owners, 0, keepdims=False)
    statics = jnp.concatenate(
        [
            stored[0, :, :band],
            stored[1, :, :band],
            sea_mask.astype(jnp.float32),
            zonal_speed,
            mixing,
            piston,
            cell_area,
            region.astype(jnp.float32),
        ],
        axis=1,
    )
    widened = padded(statics, (("tile", 0),), rim_depth)
    initial_wide = spread(
        jnp.stack([widened[:, :band], widened[:, band : 2 * band]]), "obj", owner_index
    )
    widened = widened[:, 2 * band :]
    sea_wide = widened[:, :cell_count]
    speed_wide = widened[:, cell_count : 2 * cell_count]
    mixing_wide = widened[:, 2 * cell_count : 3 * cell_count]
    offset = 3 * cell_count
    piston_wide = widened[:, offset : offset + ROWS]
    area_wide = widened[:, offset + ROWS : offset + 2 * ROWS]
    region_wide = widened[:, offset + 2 * ROWS : offset + 3 * ROWS]
    sea_east = jnp.concatenate([sea_wide[1:], jnp.zeros_like(sea_wide[:1])], axis=0)
    weights = zonal_weights(sea_wide, sea_east, speed_wide)
    row_weight, level_weight = column_weights(sea_wide, mixing_wide)
    surface_sea = sea_wide[:, :ROWS]
    targets = (lax.axis_index("obj") * groups + jnp.arange(groups, dtype=jnp.int32)).astype(
        jnp.float32
    )
    objective_seeds = area_wide[None] * (region_wide[None] == targets[:, None, None]).astype(
        jnp.float32
    )
    inner_rim = 2
    piston_inner = trim_rim(piston_wide, inner_rim, rim_depth, 0)
    sea_inner = trim_rim(surface_sea, inner_rim, rim_depth, 0)
    initial_inner = trim_rim(initial_wide, inner_rim, rim_depth, 1)
    uptake_first, slopes_first = surface_slopes(
        initial_inner[0, :, :ROWS], initial_inner[1, :, :ROWS], piston_inner, sea_inner
    )
    following = advance_rim(
        initial_wide,
        weights[:, :, :band],
        trim_rim(row_weight, inner_rim, rim_depth, 0)[:, :band],
        trim_rim(level_weight, inner_rim, rim_depth, 0)[:, :band],
        uptake_first,
    )
    _, slopes_second = surface_slopes(
        following[0, :, :ROWS], following[1, :, :ROWS], piston_inner, sea_inner
    )
    west, east = halves(as_tiles(adjoint_in), "tile", 2, rim_depth)
    span = adjoint_in.shape[2] + 2 * rim_depth

    def along(source, lead):
        pad = [(0, 0)] * source.ndim
        pad[0] = (lead, span - lead - source.shape[0])
        return jnp.pad(source, pad)

    def cells_of(source):
        pad = [(0, 0)] * source.ndim
        pad[-1] = (0, cell_count - source.shape[-1])
        return jnp.pad(source, pad)

    wide = weights.shape[1]
    stencil = as_tiles(
        jnp.stack(
            [
                along(weights[0][1:], 0),
                weights[1],
                along(weights[2][: wide - 1], 1),
                along(weights[3][: wide - 2], 2),
                row_weight,
                backward_shift(row_weight, 1),
                level_weight,
                backward_shift(level_weight, ROWS),
            ]
        )
    )
    second = jnp.moveaxis(slopes_second, 1, 0)
    first_slopes = jnp.moveaxis(trim_rim(slopes_first, 0, inner_rim, 1), 1, 0)
    slopes = as_tiles(
        cells_of(
            jnp.stack(
                [
                    jnp.moveaxis(along(second, inner_rim), 0, 1),
                    jnp.moveaxis(along(first_slopes, rim_depth), 0, 1),
                ]
            )
        )
    )
    seeds = lanes_to(objective_seeds, 128)[:, :, None, :]
    out = two_retreats(as_tiles(adjoint_in), west, east, stencil, slopes, seeds)
    return out.reshape(adjoint_in.shape)


def solution(mesh):
    placed = (
        P("obj", None, "tile", None),
        P("obj", None, "tile", None),
        P(),
        P("tile", None),
        P("tile", None),
        P("tile", None),
        P("tile", None),
        P("tile", None),
        P("tile", None),
    )
    return jax.shard_map(
        staged, mesh=mesh, in_specs=placed, out_specs=P("obj", None, "tile", None), check_vma=False
    )
```

```python
import jax
import jax.numpy as jnp
from jax import lax
from jax.sharding import PartitionSpec as P
from jax.experimental import pallas as pl
from jax.experimental.pallas import tpu as pltpu

ROWS = 32
LEVELS = 32
NEWTON = 4


DISSOCIATION_ONE = 1400.0
DISSOCIATION_TWO = 1.1
BORATE_CONSTANT = 2.5
BORON_TOTAL = 416.0
AIR_CARBON = 14.0
START_HYDROGEN = 2.0
ROW_DIFFUSION = 0.1


def padded(cells, sides, width):
    for axis, dim in sides:
        count = lax.axis_size(axis)
        head = lax.slice_in_dim(cells, 0, width, axis=dim)
        tail = lax.slice_in_dim(cells, cells.shape[dim] - width, cells.shape[dim], axis=dim)
        cells = jnp.concatenate(
            [
                lax.ppermute(tail, axis, [(i, (i + 1) % count) for i in range(count)]),
                cells,
                lax.ppermute(head, axis, [((i + 1) % count, i) for i in range(count)]),
            ],
            axis=dim,
        )
    return cells


def spread(value, axis, source):
    count = lax.axis_size(axis)
    top = count // 2
    if count < 2 or count & (count - 1):
        kept = jnp.where(lax.axis_index(axis) == source, value, 0).astype(value.dtype)
        return lax.psum(kept, axis)
    rank = jnp.bitwise_xor(lax.axis_index(axis), source)
    moved = lax.ppermute(value, axis, [(i, i ^ top) for i in range(count)])
    value = jnp.where(rank == top, moved, value)
    low = rank & (top - 1)
    received = value
    for mask in range(1, top):
        moved = lax.ppermute(value, axis, [(i, i ^ mask) for i in range(count)])
        received = jnp.where(low == mask, moved, received)
    return received


def chemistry(carbon, alkalinity, piston, surface_sea):
    hydrogen = jnp.full_like(carbon, START_HYDROGEN)
    for _ in range(NEWTON):
        square = hydrogen * hydrogen
        denominator = square + DISSOCIATION_ONE * hydrogen + DISSOCIATION_ONE * DISSOCIATION_TWO
        carbonate = carbon * DISSOCIATION_ONE * (hydrogen + 2.0 * DISSOCIATION_TWO) / denominator
        borate = BORON_TOTAL * BORATE_CONSTANT / (hydrogen + BORATE_CONSTANT)
        derivative = -carbon * DISSOCIATION_ONE * (
            square + 4.0 * DISSOCIATION_TWO * hydrogen + DISSOCIATION_ONE * DISSOCIATION_TWO
        ) / (denominator * denominator) - borate / (hydrogen + BORATE_CONSTANT)
        hydrogen = hydrogen - (carbonate + borate - alkalinity) / derivative
    square = hydrogen * hydrogen
    denominator = square + DISSOCIATION_ONE * hydrogen + DISSOCIATION_ONE * DISSOCIATION_TWO
    dissolved = carbon * square / denominator
    return surface_sea * piston * (AIR_CARBON - dissolved)


def forward_shift(source, offset):
    padding = jnp.zeros(source.shape[:-1] + (offset,), source.dtype)
    return jnp.concatenate([source[..., offset:], padding], axis=-1)


def backward_shift(source, offset):
    padding = jnp.zeros(source.shape[:-1] + (offset,), source.dtype)
    return jnp.concatenate([padding, source[..., :-offset]], axis=-1)


def column_weights(sea_float, mixing):
    cell_index = jnp.arange(LEVELS * ROWS, dtype=jnp.int32)
    row_open = (cell_index % ROWS < ROWS - 1).astype(jnp.float32)
    level_open = (cell_index // ROWS < LEVELS - 1).astype(jnp.float32)
    row_weight = ROW_DIFFUSION * row_open * sea_float * forward_shift(sea_float, 1)
    level_weight = mixing * level_open * sea_float * forward_shift(sea_float, ROWS)
    return (row_weight, level_weight)


def column_mix(source, row_weight, level_weight):
    row_flux = row_weight * (forward_shift(source, 1) - source)
    level_flux = level_weight * (forward_shift(source, ROWS) - source)
    return row_flux - backward_shift(row_flux, 1) + level_flux - backward_shift(level_flux, ROWS)


def zonal_weights(sea_float, sea_east, velocity):
    opened = sea_float * sea_east
    magnitude = jnp.abs(velocity)
    return jnp.stack(
        [
            opened * (-velocity - magnitude) / 12.0,
            opened * (7.0 * velocity + 3.0 * magnitude) / 12.0,
            opened * (7.0 * velocity - 3.0 * magnitude) / 12.0,
            opened * (magnitude - velocity) / 12.0,
        ]
    )


def trim_rim(source, keep_rim, outer_rim, dimension):
    length = source.shape[dimension] - 2 * outer_rim
    return lax.slice_in_dim(
        source, outer_rim - keep_rim, outer_rim + length + keep_rim, axis=dimension
    )


def surface_slopes(carbon, alkalinity, piston, surface_sea):

    def uptake_of(carbon_in, alkalinity_in):
        return chemistry(carbon_in, alkalinity_in, piston, surface_sea)

    uptake, pullback = jax.vjp(uptake_of, carbon, alkalinity)
    by_carbon, by_alkalinity = pullback(jnp.ones_like(carbon))
    return (uptake, jnp.stack([by_carbon, by_alkalinity]))


def advance_rim(extended, weights, row_weight, level_weight, uptake):
    length = extended.shape[1]
    face_flux = (
        weights[0, 1 : length - 2] * extended[:, 0 : length - 3]
        + weights[1, 1 : length - 2] * extended[:, 1 : length - 2]
        + weights[2, 1 : length - 2] * extended[:, 2 : length - 1]
        + weights[3, 1 : length - 2] * extended[:, 3:length]
    )
    interior = extended[:, 2 : length - 2]
    zonal_term = -(face_flux[:, 1:] - face_flux[:, :-1])
    transported = interior + zonal_term + column_mix(interior, row_weight, level_weight)
    surface_row = transported[0, :, :ROWS] + uptake
    carbon = jnp.concatenate([surface_row, transported[0, :, ROWS:]], axis=-1)
    return jnp.stack([carbon, transported[1]])


def halves(cells, axis, dim, width):
    count = lax.axis_size(axis)
    head = lax.slice_in_dim(cells, 0, width, axis=dim)
    tail = lax.slice_in_dim(cells, cells.shape[dim] - width, cells.shape[dim], axis=dim)
    west = lax.ppermute(tail, axis, [(i, (i + 1) % count) for i in range(count)])
    east = lax.ppermute(head, axis, [((i + 1) % count, i) for i in range(count)])
    return west, east


def lanes_to(source, width):
    pad = [(0, 0)] * source.ndim
    pad[-1] = (0, width - source.shape[-1])
    return jnp.pad(source, pad)


def cell_shift(x, step, lane, forward):
    if forward:
        turned = pltpu.roll(x, 128 - step, 1)
        carried = pltpu.roll(turned, 7, 0)
        return jnp.where(lane >= 128 - step, carried, turned)
    turned = pltpu.roll(x, step, 1)
    carried = pltpu.roll(turned, 1, 0)
    return jnp.where(lane < step, carried, turned)


def retreat_kernel(center_ref, west_ref, east_ref, w_ref, s_ref, seed_ref, out_ref, e_ref, f_ref):
    tracers = center_ref.shape[1]
    local = center_ref.shape[2]
    rim = west_ref.shape[2]
    lane = lax.broadcasted_iota(jnp.int32, (8, 128), 1)

    def step(src, k, stage, o):
        w = [w_ref[m, k] for m in range(8)]
        results = []
        for t in range(tracers):
            x_0 = src[t, k]
            zonal = (
                w[0] * (src[t, k + 2] - src[t, k + 1])
                + w[1] * (src[t, k + 1] - x_0)
                + w[2] * (x_0 - src[t, k - 1])
                + w[3] * (src[t, k - 1] - src[t, k - 2])
            )
            mix = (
                w[4] * (cell_shift(x_0, 1, lane, True) - x_0)
                - w[5] * (x_0 - cell_shift(x_0, 1, lane, False))
                + w[6] * (cell_shift(x_0, ROWS, lane, True) - x_0)
                - w[7] * (x_0 - cell_shift(x_0, ROWS, lane, False))
            )
            forcing = src[0, k] + seed_ref[o, k]
            results.append(x_0 + zonal + mix + s_ref[stage, t, k] * forcing)
        return results

    for o in range(center_ref.shape[0]):
        e_ref[:, rim : rim + local] = center_ref[o]
        e_ref[:, 0:rim] = west_ref[o]
        e_ref[:, rim + local : 2 * rim + local] = east_ref[o]
        for k in range(2, 2 * rim + local - 2):
            for t, value in enumerate(step(e_ref, k, 0, o)):
                f_ref[t, k] = value
        for k in range(rim, rim + local):
            for t, value in enumerate(step(f_ref, k, 1, o)):
                out_ref[o, t, k - rim] = value


def two_retreats(center, west, east, stencil, slopes, seeds):
    groups, tracers, local, sub, lanes = center.shape
    rim = west.shape[2]
    span = local + 2 * rim
    pack = 4 if groups % 4 == 0 else 1
    return pl.pallas_call(
        retreat_kernel,
        out_shape=jax.ShapeDtypeStruct(center.shape, center.dtype),
        grid=(groups // pack,),
        in_specs=[
            pl.BlockSpec((pack, tracers, local, sub, lanes), lambda g: (g, 0, 0, 0, 0)),
            pl.BlockSpec((pack, tracers, rim, sub, lanes), lambda g: (g, 0, 0, 0, 0)),
            pl.BlockSpec((pack, tracers, rim, sub, lanes), lambda g: (g, 0, 0, 0, 0)),
            pl.BlockSpec(stencil.shape, lambda g: (0, 0, 0, 0)),
            pl.BlockSpec(slopes.shape, lambda g: (0, 0, 0, 0, 0)),
            pl.BlockSpec((pack,) + seeds.shape[1:], lambda g: (g, 0, 0, 0)),
        ],
        out_specs=pl.BlockSpec((pack, tracers, local, sub, lanes), lambda g: (g, 0, 0, 0, 0)),
        scratch_shapes=[
            pltpu.VMEM((tracers, span, sub, lanes), jnp.float32),
            pltpu.VMEM((tracers, span, sub, lanes), jnp.float32),
        ],
    )(center, west, east, stencil, slopes, seeds)


def as_tiles(source):
    return source.reshape(source.shape[:-1] + (source.shape[-1] // 128, 128))


def staged(
    adjoint_in, checkpoint_store, interval, sea_mask, zonal_speed, mixing, piston, cell_area, region
):
    groups = adjoint_in.shape[0]
    cell_count = adjoint_in.shape[3]
    rim_depth = 4
    owners = lax.axis_size("obj")
    owner_index = interval[0] % owners
    band = 2 * ROWS
    stored = lax.dynamic_index_in_dim(checkpoint_store, interval[0] // owners, 0, keepdims=False)
    statics = jnp.concatenate(
        [
            stored[0, :, :band],
            stored[1, :, :band],
            sea_mask.astype(jnp.float32),
            zonal_speed,
            mixing,
            piston,
            cell_area,
            region.astype(jnp.float32),
        ],
        axis=1,
    )
    widened = padded(statics, (("tile", 0),), rim_depth)
    initial_wide = spread(
        jnp.stack([widened[:, :band], widened[:, band : 2 * band]]), "obj", owner_index
    )
    widened = widened[:, 2 * band :]
    sea_wide = widened[:, :cell_count]
    speed_wide = widened[:, cell_count : 2 * cell_count]
    mixing_wide = widened[:, 2 * cell_count : 3 * cell_count]
    offset = 3 * cell_count
    piston_wide = widened[:, offset : offset + ROWS]
    area_wide = widened[:, offset + ROWS : offset + 2 * ROWS]
    region_wide = widened[:, offset + 2 * ROWS : offset + 3 * ROWS]
    sea_east = jnp.concatenate([sea_wide[1:], jnp.zeros_like(sea_wide[:1])], axis=0)
    weights = zonal_weights(sea_wide, sea_east, speed_wide)
    row_weight, level_weight = column_weights(sea_wide, mixing_wide)
    surface_sea = sea_wide[:, :ROWS]
    targets = (lax.axis_index("obj") * groups + jnp.arange(groups, dtype=jnp.int32)).astype(
        jnp.float32
    )
    objective_seeds = area_wide[None] * (region_wide[None] == targets[:, None, None]).astype(
        jnp.float32
    )
    inner_rim = 2
    piston_inner = trim_rim(piston_wide, inner_rim, rim_depth, 0)
    sea_inner = trim_rim(surface_sea, inner_rim, rim_depth, 0)
    initial_inner = trim_rim(initial_wide, inner_rim, rim_depth, 1)
    uptake_first, slopes_first = surface_slopes(
        initial_inner[0, :, :ROWS], initial_inner[1, :, :ROWS], piston_inner, sea_inner
    )
    following = advance_rim(
        initial_wide,
        weights[:, :, :band],
        trim_rim(row_weight, inner_rim, rim_depth, 0)[:, :band],
        trim_rim(level_weight, inner_rim, rim_depth, 0)[:, :band],
        uptake_first,
    )
    _, slopes_second = surface_slopes(
        following[0, :, :ROWS], following[1, :, :ROWS], piston_inner, sea_inner
    )
    west, east = halves(as_tiles(adjoint_in), "tile", 2, rim_depth)
    span = adjoint_in.shape[2] + 2 * rim_depth

    def along(source, lead):
        pad = [(0, 0)] * source.ndim
        pad[0] = (lead, span - lead - source.shape[0])
        return jnp.pad(source, pad)

    def cells_of(source):
        pad = [(0, 0)] * source.ndim
        pad[-1] = (0, cell_count - source.shape[-1])
        return jnp.pad(source, pad)

    wide = weights.shape[1]
    stencil = as_tiles(
        jnp.stack(
            [
                along(weights[0][1:], 0),
                weights[1],
                along(weights[2][: wide - 1], 1),
                along(weights[3][: wide - 2], 2),
                row_weight,
                backward_shift(row_weight, 1),
                level_weight,
                backward_shift(level_weight, ROWS),
            ]
        )
    )
    second = jnp.moveaxis(slopes_second, 1, 0)
    first_slopes = jnp.moveaxis(trim_rim(slopes_first, 0, inner_rim, 1), 1, 0)
    slopes = as_tiles(
        cells_of(
            jnp.stack(
                [
                    jnp.moveaxis(along(second, inner_rim), 0, 1),
                    jnp.moveaxis(along(first_slopes, rim_depth), 0, 1),
                ]
            )
        )
    )
    seeds = lanes_to(objective_seeds, 128)[:, :, None, :]
    out = two_retreats(as_tiles(adjoint_in), west, east, stencil, slopes, seeds)
    return out.reshape(adjoint_in.shape)


def solution(mesh):
    placed = (
        P("obj", None, "tile", None),
        P("obj", None, "tile", None),
        P(),
        P("tile", None),
        P("tile", None),
        P("tile", None),
        P("tile", None),
        P("tile", None),
        P("tile", None),
    )
    return jax.shard_map(
        staged, mesh=mesh, in_specs=placed, out_specs=P("obj", None, "tile", None), check_vma=False
    )
```

```python
import jax
import jax.numpy as jnp
from jax import lax
from jax.sharding import PartitionSpec as P
from jax.experimental import pallas as pl
from jax.experimental.pallas import tpu as pltpu

ROWS = 32
LEVELS = 32
NEWTON = 4


DISSOCIATION_ONE = 1400.0
DISSOCIATION_TWO = 1.1
BORATE_CONSTANT = 2.5
BORON_TOTAL = 416.0
AIR_CARBON = 14.0
START_HYDROGEN = 2.0
ROW_DIFFUSION = 0.1


def padded(cells, sides, width):
    for axis, dim in sides:
        count = lax.axis_size(axis)
        head = lax.slice_in_dim(cells, 0, width, axis=dim)
        tail = lax.slice_in_dim(cells, cells.shape[dim] - width, cells.shape[dim], axis=dim)
        cells = jnp.concatenate(
            [
                lax.ppermute(tail, axis, [(i, (i + 1) % count) for i in range(count)]),
                cells,
                lax.ppermute(head, axis, [((i + 1) % count, i) for i in range(count)]),
            ],
            axis=dim,
        )
    return cells


def spread(value, axis, source):
    count = lax.axis_size(axis)
    top = count // 2
    if count < 2 or count & (count - 1):
        kept = jnp.where(lax.axis_index(axis) == source, value, 0).astype(value.dtype)
        return lax.psum(kept, axis)
    rank = jnp.bitwise_xor(lax.axis_index(axis), source)
    moved = lax.ppermute(value, axis, [(i, i ^ top) for i in range(count)])
    value = jnp.where(rank == top, moved, value)
    low = rank & (top - 1)
    received = value
    for mask in range(1, top):
        moved = lax.ppermute(value, axis, [(i, i ^ mask) for i in range(count)])
        received = jnp.where(low == mask, moved, received)
    return received


def chemistry(carbon, alkalinity, piston, surface_sea):
    hydrogen = jnp.full_like(carbon, START_HYDROGEN)
    for _ in range(NEWTON):
        square = hydrogen * hydrogen
        denominator = square + DISSOCIATION_ONE * hydrogen + DISSOCIATION_ONE * DISSOCIATION_TWO
        carbonate = carbon * DISSOCIATION_ONE * (hydrogen + 2.0 * DISSOCIATION_TWO) / denominator
        borate = BORON_TOTAL * BORATE_CONSTANT / (hydrogen + BORATE_CONSTANT)
        derivative = -carbon * DISSOCIATION_ONE * (
            square + 4.0 * DISSOCIATION_TWO * hydrogen + DISSOCIATION_ONE * DISSOCIATION_TWO
        ) / (denominator * denominator) - borate / (hydrogen + BORATE_CONSTANT)
        hydrogen = hydrogen - (carbonate + borate - alkalinity) / derivative
    square = hydrogen * hydrogen
    denominator = square + DISSOCIATION_ONE * hydrogen + DISSOCIATION_ONE * DISSOCIATION_TWO
    dissolved = carbon * square / denominator
    return surface_sea * piston * (AIR_CARBON - dissolved)


def forward_shift(source, offset):
    padding = jnp.zeros(source.shape[:-1] + (offset,), source.dtype)
    return jnp.concatenate([source[..., offset:], padding], axis=-1)


def backward_shift(source, offset):
    padding = jnp.zeros(source.shape[:-1] + (offset,), source.dtype)
    return jnp.concatenate([padding, source[..., :-offset]], axis=-1)


def column_weights(sea_float, mixing):
    cell_index = jnp.arange(LEVELS * ROWS, dtype=jnp.int32)
    row_open = (cell_index % ROWS < ROWS - 1).astype(jnp.float32)
    level_open = (cell_index // ROWS < LEVELS - 1).astype(jnp.float32)
    row_weight = ROW_DIFFUSION * row_open * sea_float * forward_shift(sea_float, 1)
    level_weight = mixing * level_open * sea_float * forward_shift(sea_float, ROWS)
    return (row_weight, level_weight)


def column_mix(source, row_weight, level_weight):
    row_flux = row_weight * (forward_shift(source, 1) - source)
    level_flux = level_weight * (forward_shift(source, ROWS) - source)
    return row_flux - backward_shift(row_flux, 1) + level_flux - backward_shift(level_flux, ROWS)


def zonal_weights(sea_float, sea_east, velocity):
    opened = sea_float * sea_east
    magnitude = jnp.abs(velocity)
    return jnp.stack(
        [
            opened * (-velocity - magnitude) / 12.0,
            opened * (7.0 * velocity + 3.0 * magnitude) / 12.0,
            opened * (7.0 * velocity - 3.0 * magnitude) / 12.0,
            opened * (magnitude - velocity) / 12.0,
        ]
    )


def trim_rim(source, keep_rim, outer_rim, dimension):
    length = source.shape[dimension] - 2 * outer_rim
    return lax.slice_in_dim(
        source, outer_rim - keep_rim, outer_rim + length + keep_rim, axis=dimension
    )


def surface_slopes(carbon, alkalinity, piston, surface_sea):

    def uptake_of(carbon_in, alkalinity_in):
        return chemistry(carbon_in, alkalinity_in, piston, surface_sea)

    uptake, pullback = jax.vjp(uptake_of, carbon, alkalinity)
    by_carbon, by_alkalinity = pullback(jnp.ones_like(carbon))
    return (uptake, jnp.stack([by_carbon, by_alkalinity]))


def advance_rim(extended, weights, row_weight, level_weight, uptake):
    length = extended.shape[1]
    face_flux = (
        weights[0, 1 : length - 2] * extended[:, 0 : length - 3]
        + weights[1, 1 : length - 2] * extended[:, 1 : length - 2]
        + weights[2, 1 : length - 2] * extended[:, 2 : length - 1]
        + weights[3, 1 : length - 2] * extended[:, 3:length]
    )
    interior = extended[:, 2 : length - 2]
    zonal_term = -(face_flux[:, 1:] - face_flux[:, :-1])
    transported = interior + zonal_term + column_mix(interior, row_weight, level_weight)
    surface_row = transported[0, :, :ROWS] + uptake
    carbon = jnp.concatenate([surface_row, transported[0, :, ROWS:]], axis=-1)
    return jnp.stack([carbon, transported[1]])


def halves(cells, axis, dim, width):
    count = lax.axis_size(axis)
    head = lax.slice_in_dim(cells, 0, width, axis=dim)
    tail = lax.slice_in_dim(cells, cells.shape[dim] - width, cells.shape[dim], axis=dim)
    west = lax.ppermute(tail, axis, [(i, (i + 1) % count) for i in range(count)])
    east = lax.ppermute(head, axis, [((i + 1) % count, i) for i in range(count)])
    return west, east


def lanes_to(source, width):
    pad = [(0, 0)] * source.ndim
    pad[-1] = (0, width - source.shape[-1])
    return jnp.pad(source, pad)


def cell_shift(x, step, lane, forward):
    if forward:
        turned = pltpu.roll(x, 128 - step, 1)
        carried = pltpu.roll(turned, 7, 0)
        return jnp.where(lane >= 128 - step, carried, turned)
    turned = pltpu.roll(x, step, 1)
    carried = pltpu.roll(turned, 1, 0)
    return jnp.where(lane < step, carried, turned)


def retreat_kernel(center_ref, west_ref, east_ref, w_ref, s_ref, seed_ref, out_ref, e_ref, f_ref):
    tracers = center_ref.shape[1]
    local = center_ref.shape[2]
    rim = west_ref.shape[2]
    lane = lax.broadcasted_iota(jnp.int32, (8, 128), 1)

    def step(src, k, stage, o):
        w = [w_ref[m, k] for m in range(8)]
        results = []
        for t in range(tracers):
            x_0 = src[t, k]
            zonal = (
                w[0] * (src[t, k + 2] - src[t, k + 1])
                + w[1] * (src[t, k + 1] - x_0)
                + w[2] * (x_0 - src[t, k - 1])
                + w[3] * (src[t, k - 1] - src[t, k - 2])
            )
            mix = (
                w[4] * (cell_shift(x_0, 1, lane, True) - x_0)
                - w[5] * (x_0 - cell_shift(x_0, 1, lane, False))
                + w[6] * (cell_shift(x_0, ROWS, lane, True) - x_0)
                - w[7] * (x_0 - cell_shift(x_0, ROWS, lane, False))
            )
            forcing = src[0, k] + seed_ref[o, k]
            results.append(x_0 + zonal + mix + s_ref[stage, t, k] * forcing)
        return results

    for o in range(center_ref.shape[0]):
        e_ref[:, rim : rim + local] = center_ref[o]
        e_ref[:, 0:rim] = west_ref[o]
        e_ref[:, rim + local : 2 * rim + local] = east_ref[o]
        for k in range(2, 2 * rim + local - 2):
            for t, value in enumerate(step(e_ref, k, 0, o)):
                f_ref[t, k] = value
        for q in range(0, local, 8):
            rows = [step(f_ref, rim + q + i, 1, o) for i in range(8)]
            for t in range(tracers):
                stacked = jnp.stack([row[t] for row in rows])
                out_ref[o, t, q : q + 8, :] = stacked.reshape(8, stacked.shape[1] * stacked.shape[2])


def two_retreats(center, west, east, stencil, slopes, seeds):
    groups, tracers, local, sub, lanes = center.shape
    rim = west.shape[2]
    span = local + 2 * rim
    pack = 4 if groups % 4 == 0 else 1
    return pl.pallas_call(
        retreat_kernel,
        out_shape=jax.ShapeDtypeStruct((groups, tracers, local, sub * lanes), center.dtype),
        grid=(groups // pack,),
        in_specs=[
            pl.BlockSpec((pack, tracers, local, sub, lanes), lambda g: (g, 0, 0, 0, 0)),
            pl.BlockSpec((pack, tracers, rim, sub, lanes), lambda g: (g, 0, 0, 0, 0)),
            pl.BlockSpec((pack, tracers, rim, sub, lanes), lambda g: (g, 0, 0, 0, 0)),
            pl.BlockSpec(stencil.shape, lambda g: (0, 0, 0, 0)),
            pl.BlockSpec(slopes.shape, lambda g: (0, 0, 0, 0, 0)),
            pl.BlockSpec((pack,) + seeds.shape[1:], lambda g: (g, 0, 0, 0)),
        ],
        out_specs=pl.BlockSpec((pack, tracers, local, sub * lanes), lambda g: (g, 0, 0, 0)),
        scratch_shapes=[
            pltpu.VMEM((tracers, span, sub, lanes), jnp.float32),
            pltpu.VMEM((tracers, span, sub, lanes), jnp.float32),
        ],
    )(center, west, east, stencil, slopes, seeds)


def as_tiles(source):
    return source.reshape(source.shape[:-1] + (source.shape[-1] // 128, 128))


def staged(
    adjoint_in, checkpoint_store, interval, sea_mask, zonal_speed, mixing, piston, cell_area, region
):
    groups = adjoint_in.shape[0]
    cell_count = adjoint_in.shape[3]
    rim_depth = 4
    owners = lax.axis_size("obj")
    owner_index = interval[0] % owners
    band = 2 * ROWS
    stored = lax.dynamic_index_in_dim(checkpoint_store, interval[0] // owners, 0, keepdims=False)
    band_wide = padded(
        jnp.concatenate([stored[0, :, :band], stored[1, :, :band]], axis=1),
        (("tile", 0),),
        rim_depth,
    )
    initial_wide = spread(
        jnp.stack([band_wide[:, :band], band_wide[:, band : 2 * band]]), "obj", owner_index
    )
    statics = jnp.concatenate(
        [
            sea_mask.astype(jnp.float32),
            zonal_speed,
            mixing,
            piston,
            cell_area,
            region.astype(jnp.float32),
        ],
        axis=1,
    )
    widened = padded(statics, (("tile", 0),), rim_depth)
    sea_wide = widened[:, :cell_count]
    speed_wide = widened[:, cell_count : 2 * cell_count]
    mixing_wide = widened[:, 2 * cell_count : 3 * cell_count]
    offset = 3 * cell_count
    piston_wide = widened[:, offset : offset + ROWS]
    area_wide = widened[:, offset + ROWS : offset + 2 * ROWS]
    region_wide = widened[:, offset + 2 * ROWS : offset + 3 * ROWS]
    sea_east = jnp.concatenate([sea_wide[1:], jnp.zeros_like(sea_wide[:1])], axis=0)
    weights = zonal_weights(sea_wide, sea_east, speed_wide)
    row_weight, level_weight = column_weights(sea_wide, mixing_wide)
    surface_sea = sea_wide[:, :ROWS]
    targets = (lax.axis_index("obj") * groups + jnp.arange(groups, dtype=jnp.int32)).astype(
        jnp.float32
    )
    objective_seeds = area_wide[None] * (region_wide[None] == targets[:, None, None]).astype(
        jnp.float32
    )
    inner_rim = 2
    piston_inner = trim_rim(piston_wide, inner_rim, rim_depth, 0)
    sea_inner = trim_rim(surface_sea, inner_rim, rim_depth, 0)
    initial_inner = trim_rim(initial_wide, inner_rim, rim_depth, 1)
    uptake_first, slopes_first = surface_slopes(
        initial_inner[0, :, :ROWS], initial_inner[1, :, :ROWS], piston_inner, sea_inner
    )
    following = advance_rim(
        initial_wide,
        weights[:, :, :band],
        trim_rim(row_weight, inner_rim, rim_depth, 0)[:, :band],
        trim_rim(level_weight, inner_rim, rim_depth, 0)[:, :band],
        uptake_first,
    )
    _, slopes_second = surface_slopes(
        following[0, :, :ROWS], following[1, :, :ROWS], piston_inner, sea_inner
    )
    west, east = halves(as_tiles(adjoint_in), "tile", 2, rim_depth)
    span = adjoint_in.shape[2] + 2 * rim_depth

    def along(source, lead):
        pad = [(0, 0)] * source.ndim
        pad[0] = (lead, span - lead - source.shape[0])
        return jnp.pad(source, pad)

    def cells_of(source):
        pad = [(0, 0)] * source.ndim
        pad[-1] = (0, cell_count - source.shape[-1])
        return jnp.pad(source, pad)

    wide = weights.shape[1]
    stencil = as_tiles(
        jnp.stack(
            [
                along(weights[0][1:], 0),
                weights[1],
                along(weights[2][: wide - 1], 1),
                along(weights[3][: wide - 2], 2),
                row_weight,
                backward_shift(row_weight, 1),
                level_weight,
                backward_shift(level_weight, ROWS),
            ]
        )
    )
    second = jnp.moveaxis(slopes_second, 1, 0)
    first_slopes = jnp.moveaxis(trim_rim(slopes_first, 0, inner_rim, 1), 1, 0)
    slopes = as_tiles(
        cells_of(
            jnp.stack(
                [
                    jnp.moveaxis(along(second, inner_rim), 0, 1),
                    jnp.moveaxis(along(first_slopes, rim_depth), 0, 1),
                ]
            )
        )
    )
    seeds = lanes_to(objective_seeds, 128)[:, :, None, :]
    return two_retreats(as_tiles(adjoint_in), west, east, stencil, slopes, seeds)


def solution(mesh):
    placed = (
        P("obj", None, "tile", None),
        P("obj", None, "tile", None),
        P(),
        P("tile", None),
        P("tile", None),
        P("tile", None),
        P("tile", None),
        P("tile", None),
        P("tile", None),
    )
    return jax.shard_map(
        staged, mesh=mesh, in_specs=placed, out_specs=P("obj", None, "tile", None), check_vma=False
    )
```

```python
import jax
import jax.numpy as jnp
from jax import lax
from jax.sharding import PartitionSpec as P
from jax.experimental import pallas as pl
from jax.experimental.pallas import tpu as pltpu

ROWS = 32
LEVELS = 32
NEWTON = 4


DISSOCIATION_ONE = 1400.0
DISSOCIATION_TWO = 1.1
BORATE_CONSTANT = 2.5
BORON_TOTAL = 416.0
AIR_CARBON = 14.0
START_HYDROGEN = 2.0
ROW_DIFFUSION = 0.1


def padded(cells, sides, width):
    for axis, dim in sides:
        count = lax.axis_size(axis)
        head = lax.slice_in_dim(cells, 0, width, axis=dim)
        tail = lax.slice_in_dim(cells, cells.shape[dim] - width, cells.shape[dim], axis=dim)
        cells = jnp.concatenate(
            [
                lax.ppermute(tail, axis, [(i, (i + 1) % count) for i in range(count)]),
                cells,
                lax.ppermute(head, axis, [((i + 1) % count, i) for i in range(count)]),
            ],
            axis=dim,
        )
    return cells


def spread(value, axis, source):
    count = lax.axis_size(axis)
    top = count // 2
    if count < 2 or count & (count - 1):
        kept = jnp.where(lax.axis_index(axis) == source, value, 0).astype(value.dtype)
        return lax.psum(kept, axis)
    rank = jnp.bitwise_xor(lax.axis_index(axis), source)
    moved = lax.ppermute(value, axis, [(i, i ^ top) for i in range(count)])
    value = jnp.where(rank == top, moved, value)
    low = rank & (top - 1)
    received = value
    for mask in range(1, top):
        moved = lax.ppermute(value, axis, [(i, i ^ mask) for i in range(count)])
        received = jnp.where(low == mask, moved, received)
    return received


def chemistry(carbon, alkalinity, piston, surface_sea):
    hydrogen = jnp.full_like(carbon, START_HYDROGEN)
    for _ in range(NEWTON):
        square = hydrogen * hydrogen
        denominator = square + DISSOCIATION_ONE * hydrogen + DISSOCIATION_ONE * DISSOCIATION_TWO
        carbonate = carbon * DISSOCIATION_ONE * (hydrogen + 2.0 * DISSOCIATION_TWO) / denominator
        borate = BORON_TOTAL * BORATE_CONSTANT / (hydrogen + BORATE_CONSTANT)
        derivative = -carbon * DISSOCIATION_ONE * (
            square + 4.0 * DISSOCIATION_TWO * hydrogen + DISSOCIATION_ONE * DISSOCIATION_TWO
        ) / (denominator * denominator) - borate / (hydrogen + BORATE_CONSTANT)
        hydrogen = hydrogen - (carbonate + borate - alkalinity) / derivative
    square = hydrogen * hydrogen
    denominator = square + DISSOCIATION_ONE * hydrogen + DISSOCIATION_ONE * DISSOCIATION_TWO
    dissolved = carbon * square / denominator
    return surface_sea * piston * (AIR_CARBON - dissolved)


def forward_shift(source, offset):
    padding = jnp.zeros(source.shape[:-1] + (offset,), source.dtype)
    return jnp.concatenate([source[..., offset:], padding], axis=-1)


def backward_shift(source, offset):
    padding = jnp.zeros(source.shape[:-1] + (offset,), source.dtype)
    return jnp.concatenate([padding, source[..., :-offset]], axis=-1)


def column_weights(sea_float, mixing):
    cell_index = jnp.arange(LEVELS * ROWS, dtype=jnp.int32)
    row_open = (cell_index % ROWS < ROWS - 1).astype(jnp.float32)
    level_open = (cell_index // ROWS < LEVELS - 1).astype(jnp.float32)
    row_weight = ROW_DIFFUSION * row_open * sea_float * forward_shift(sea_float, 1)
    level_weight = mixing * level_open * sea_float * forward_shift(sea_float, ROWS)
    return (row_weight, level_weight)


def column_mix(source, row_weight, level_weight):
    row_flux = row_weight * (forward_shift(source, 1) - source)
    level_flux = level_weight * (forward_shift(source, ROWS) - source)
    return row_flux - backward_shift(row_flux, 1) + level_flux - backward_shift(level_flux, ROWS)


def zonal_weights(sea_float, sea_east, velocity):
    opened = sea_float * sea_east
    magnitude = jnp.abs(velocity)
    return jnp.stack(
        [
            opened * (-velocity - magnitude) / 12.0,
            opened * (7.0 * velocity + 3.0 * magnitude) / 12.0,
            opened * (7.0 * velocity - 3.0 * magnitude) / 12.0,
            opened * (magnitude - velocity) / 12.0,
        ]
    )


def trim_rim(source, keep_rim, outer_rim, dimension):
    length = source.shape[dimension] - 2 * outer_rim
    return lax.slice_in_dim(
        source, outer_rim - keep_rim, outer_rim + length + keep_rim, axis=dimension
    )


def surface_slopes(carbon, alkalinity, piston, surface_sea):

    def uptake_of(carbon_in, alkalinity_in):
        return chemistry(carbon_in, alkalinity_in, piston, surface_sea)

    uptake, pullback = jax.vjp(uptake_of, carbon, alkalinity)
    by_carbon, by_alkalinity = pullback(jnp.ones_like(carbon))
    return (uptake, jnp.stack([by_carbon, by_alkalinity]))


def advance_rim(extended, weights, row_weight, level_weight, uptake):
    length = extended.shape[1]
    face_flux = (
        weights[0, 1 : length - 2] * extended[:, 0 : length - 3]
        + weights[1, 1 : length - 2] * extended[:, 1 : length - 2]
        + weights[2, 1 : length - 2] * extended[:, 2 : length - 1]
        + weights[3, 1 : length - 2] * extended[:, 3:length]
    )
    interior = extended[:, 2 : length - 2]
    zonal_term = -(face_flux[:, 1:] - face_flux[:, :-1])
    transported = interior + zonal_term + column_mix(interior, row_weight, level_weight)
    surface_row = transported[0, :, :ROWS] + uptake
    carbon = jnp.concatenate([surface_row, transported[0, :, ROWS:]], axis=-1)
    return jnp.stack([carbon, transported[1]])


def halves(cells, axis, dim, width):
    count = lax.axis_size(axis)
    head = lax.slice_in_dim(cells, 0, width, axis=dim)
    tail = lax.slice_in_dim(cells, cells.shape[dim] - width, cells.shape[dim], axis=dim)
    west = lax.ppermute(tail, axis, [(i, (i + 1) % count) for i in range(count)])
    east = lax.ppermute(head, axis, [((i + 1) % count, i) for i in range(count)])
    return west, east


def lanes_to(source, width):
    pad = [(0, 0)] * source.ndim
    pad[-1] = (0, width - source.shape[-1])
    return jnp.pad(source, pad)


def cell_shift(x, step, lane, forward):
    if forward:
        turned = pltpu.roll(x, 128 - step, 1)
        carried = pltpu.roll(turned, 7, 0)
        return jnp.where(lane >= 128 - step, carried, turned)
    turned = pltpu.roll(x, step, 1)
    carried = pltpu.roll(turned, 1, 0)
    return jnp.where(lane < step, carried, turned)


def retreat_kernel(center_ref, west_ref, east_ref, w_ref, s_ref, seed_ref, out_ref, e_ref, f_ref):
    tracers = center_ref.shape[1]
    local = center_ref.shape[2]
    rim = west_ref.shape[2]
    lane = lax.broadcasted_iota(jnp.int32, (8, 128), 1)

    def step(src, k, stage, o):
        w = [w_ref[m, k] for m in range(8)]
        results = []
        for t in range(tracers):
            x_0 = src[t, k]
            zonal = (
                w[0] * (src[t, k + 2] - src[t, k + 1])
                + w[1] * (src[t, k + 1] - x_0)
                + w[2] * (x_0 - src[t, k - 1])
                + w[3] * (src[t, k - 1] - src[t, k - 2])
            )
            mix = (
                w[4] * (cell_shift(x_0, 1, lane, True) - x_0)
                - w[5] * (x_0 - cell_shift(x_0, 1, lane, False))
                + w[6] * (cell_shift(x_0, ROWS, lane, True) - x_0)
                - w[7] * (x_0 - cell_shift(x_0, ROWS, lane, False))
            )
            forcing = src[0, k] + seed_ref[o, k]
            results.append(x_0 + zonal + mix + s_ref[stage, t, k] * forcing)
        return results

    for o in range(center_ref.shape[0]):
        e_ref[:, rim : rim + local] = center_ref[o]
        e_ref[:, 0:rim] = west_ref[o]
        e_ref[:, rim + local : 2 * rim + local] = east_ref[o]
        for k in range(2, 2 * rim + local - 2):
            for t, value in enumerate(step(e_ref, k, 0, o)):
                f_ref[t, k] = value
        for q in range(0, local, 8):
            rows = [step(f_ref, rim + q + i, 1, o) for i in range(8)]
            for t in range(tracers):
                stacked = jnp.stack([row[t] for row in rows])
                out_ref[o, t, q : q + 8, :] = stacked.reshape(8, stacked.shape[1] * stacked.shape[2])


def two_retreats(center, west, east, stencil, slopes, seeds):
    groups, tracers, local, sub, lanes = center.shape
    rim = west.shape[2]
    span = local + 2 * rim
    pack = 8 if groups % 8 == 0 else 1
    return pl.pallas_call(
        retreat_kernel,
        out_shape=jax.ShapeDtypeStruct((groups, tracers, local, sub * lanes), center.dtype),
        grid=(groups // pack,),
        in_specs=[
            pl.BlockSpec((pack, tracers, local, sub, lanes), lambda g: (g, 0, 0, 0, 0)),
            pl.BlockSpec((pack, tracers, rim, sub, lanes), lambda g: (g, 0, 0, 0, 0)),
            pl.BlockSpec((pack, tracers, rim, sub, lanes), lambda g: (g, 0, 0, 0, 0)),
            pl.BlockSpec(stencil.shape, lambda g: (0, 0, 0, 0)),
            pl.BlockSpec(slopes.shape, lambda g: (0, 0, 0, 0, 0)),
            pl.BlockSpec((pack,) + seeds.shape[1:], lambda g: (g, 0, 0, 0)),
        ],
        out_specs=pl.BlockSpec((pack, tracers, local, sub * lanes), lambda g: (g, 0, 0, 0)),
        scratch_shapes=[
            pltpu.VMEM((tracers, span, sub, lanes), jnp.float32),
            pltpu.VMEM((tracers, span, sub, lanes), jnp.float32),
        ],
    )(center, west, east, stencil, slopes, seeds)


def as_tiles(source):
    return source.reshape(source.shape[:-1] + (source.shape[-1] // 128, 128))


def staged(
    adjoint_in, checkpoint_store, interval, sea_mask, zonal_speed, mixing, piston, cell_area, region
):
    groups = adjoint_in.shape[0]
    cell_count = adjoint_in.shape[3]
    rim_depth = 4
    owners = lax.axis_size("obj")
    owner_index = interval[0] % owners
    band = 2 * ROWS
    stored = lax.dynamic_index_in_dim(checkpoint_store, interval[0] // owners, 0, keepdims=False)
    statics = jnp.concatenate(
        [
            stored[0, :, :band],
            stored[1, :, :band],
            sea_mask.astype(jnp.float32),
            zonal_speed,
            mixing,
            piston,
            cell_area,
            region.astype(jnp.float32),
        ],
        axis=1,
    )
    widened = padded(statics, (("tile", 0),), rim_depth)
    initial_wide = spread(
        jnp.stack([widened[:, :band], widened[:, band : 2 * band]]), "obj", owner_index
    )
    widened = widened[:, 2 * band :]
    sea_wide = widened[:, :cell_count]
    speed_wide = widened[:, cell_count : 2 * cell_count]
    mixing_wide = widened[:, 2 * cell_count : 3 * cell_count]
    offset = 3 * cell_count
    piston_wide = widened[:, offset : offset + ROWS]
    area_wide = widened[:, offset + ROWS : offset + 2 * ROWS]
    region_wide = widened[:, offset + 2 * ROWS : offset + 3 * ROWS]
    sea_east = jnp.concatenate([sea_wide[1:], jnp.zeros_like(sea_wide[:1])], axis=0)
    weights = zonal_weights(sea_wide, sea_east, speed_wide)
    row_weight, level_weight = column_weights(sea_wide, mixing_wide)
    surface_sea = sea_wide[:, :ROWS]
    targets = (lax.axis_index("obj") * groups + jnp.arange(groups, dtype=jnp.int32)).astype(
        jnp.float32
    )
    objective_seeds = area_wide[None] * (region_wide[None] == targets[:, None, None]).astype(
        jnp.float32
    )
    inner_rim = 2
    piston_inner = trim_rim(piston_wide, inner_rim, rim_depth, 0)
    sea_inner = trim_rim(surface_sea, inner_rim, rim_depth, 0)
    initial_inner = trim_rim(initial_wide, inner_rim, rim_depth, 1)
    uptake_first, slopes_first = surface_slopes(
        initial_inner[0, :, :ROWS], initial_inner[1, :, :ROWS], piston_inner, sea_inner
    )
    following = advance_rim(
        initial_wide,
        weights[:, :, :band],
        trim_rim(row_weight, inner_rim, rim_depth, 0)[:, :band],
        trim_rim(level_weight, inner_rim, rim_depth, 0)[:, :band],
        uptake_first,
    )
    _, slopes_second = surface_slopes(
        following[0, :, :ROWS], following[1, :, :ROWS], piston_inner, sea_inner
    )
    west, east = halves(as_tiles(adjoint_in), "tile", 2, rim_depth)
    span = adjoint_in.shape[2] + 2 * rim_depth

    def along(source, lead):
        pad = [(0, 0)] * source.ndim
        pad[0] = (lead, span - lead - source.shape[0])
        return jnp.pad(source, pad)

    def cells_of(source):
        pad = [(0, 0)] * source.ndim
        pad[-1] = (0, cell_count - source.shape[-1])
        return jnp.pad(source, pad)

    wide = weights.shape[1]
    stencil = as_tiles(
        jnp.stack(
            [
                along(weights[0][1:], 0),
                weights[1],
                along(weights[2][: wide - 1], 1),
                along(weights[3][: wide - 2], 2),
                row_weight,
                backward_shift(row_weight, 1),
                level_weight,
                backward_shift(level_weight, ROWS),
            ]
        )
    )
    second = jnp.moveaxis(slopes_second, 1, 0)
    first_slopes = jnp.moveaxis(trim_rim(slopes_first, 0, inner_rim, 1), 1, 0)
    slopes = as_tiles(
        cells_of(
            jnp.stack(
                [
                    jnp.moveaxis(along(second, inner_rim), 0, 1),
                    jnp.moveaxis(along(first_slopes, rim_depth), 0, 1),
                ]
            )
        )
    )
    seeds = lanes_to(objective_seeds, 128)[:, :, None, :]
    return two_retreats(as_tiles(adjoint_in), west, east, stencil, slopes, seeds)


def solution(mesh):
    placed = (
        P("obj", None, "tile", None),
        P("obj", None, "tile", None),
        P(),
        P("tile", None),
        P("tile", None),
        P("tile", None),
        P("tile", None),
        P("tile", None),
        P("tile", None),
    )
    return jax.shard_map(
        staged, mesh=mesh, in_specs=placed, out_specs=P("obj", None, "tile", None), check_vma=False
    )
```

```python
import jax
import jax.numpy as jnp
from jax import lax
from jax.sharding import PartitionSpec as P
from jax.experimental import pallas as pl
from jax.experimental.pallas import tpu as pltpu

ROWS = 32
LEVELS = 32
NEWTON = 4


DISSOCIATION_ONE = 1400.0
DISSOCIATION_TWO = 1.1
BORATE_CONSTANT = 2.5
BORON_TOTAL = 416.0
AIR_CARBON = 14.0
START_HYDROGEN = 2.0
ROW_DIFFUSION = 0.1


def padded(cells, sides, width):
    for axis, dim in sides:
        count = lax.axis_size(axis)
        head = lax.slice_in_dim(cells, 0, width, axis=dim)
        tail = lax.slice_in_dim(cells, cells.shape[dim] - width, cells.shape[dim], axis=dim)
        cells = jnp.concatenate(
            [
                lax.ppermute(tail, axis, [(i, (i + 1) % count) for i in range(count)]),
                cells,
                lax.ppermute(head, axis, [((i + 1) % count, i) for i in range(count)]),
            ],
            axis=dim,
        )
    return cells


def spread(value, axis, source):
    count = lax.axis_size(axis)
    top = count // 2
    if count < 2 or count & (count - 1):
        kept = jnp.where(lax.axis_index(axis) == source, value, 0).astype(value.dtype)
        return lax.psum(kept, axis)
    rank = jnp.bitwise_xor(lax.axis_index(axis), source)
    moved = lax.ppermute(value, axis, [(i, i ^ top) for i in range(count)])
    value = jnp.where(rank == top, moved, value)
    low = rank & (top - 1)
    received = value
    for mask in range(1, top):
        moved = lax.ppermute(value, axis, [(i, i ^ mask) for i in range(count)])
        received = jnp.where(low == mask, moved, received)
    return received


def chemistry(carbon, alkalinity, piston, surface_sea):
    hydrogen = jnp.full_like(carbon, START_HYDROGEN)
    for _ in range(NEWTON):
        square = hydrogen * hydrogen
        denominator = square + DISSOCIATION_ONE * hydrogen + DISSOCIATION_ONE * DISSOCIATION_TWO
        carbonate = carbon * DISSOCIATION_ONE * (hydrogen + 2.0 * DISSOCIATION_TWO) / denominator
        borate = BORON_TOTAL * BORATE_CONSTANT / (hydrogen + BORATE_CONSTANT)
        derivative = -carbon * DISSOCIATION_ONE * (
            square + 4.0 * DISSOCIATION_TWO * hydrogen + DISSOCIATION_ONE * DISSOCIATION_TWO
        ) / (denominator * denominator) - borate / (hydrogen + BORATE_CONSTANT)
        hydrogen = hydrogen - (carbonate + borate - alkalinity) / derivative
    square = hydrogen * hydrogen
    denominator = square + DISSOCIATION_ONE * hydrogen + DISSOCIATION_ONE * DISSOCIATION_TWO
    dissolved = carbon * square / denominator
    return surface_sea * piston * (AIR_CARBON - dissolved)


def forward_shift(source, offset):
    padding = jnp.zeros(source.shape[:-1] + (offset,), source.dtype)
    return jnp.concatenate([source[..., offset:], padding], axis=-1)


def backward_shift(source, offset):
    padding = jnp.zeros(source.shape[:-1] + (offset,), source.dtype)
    return jnp.concatenate([padding, source[..., :-offset]], axis=-1)


def column_weights(sea_float, mixing):
    cell_index = jnp.arange(LEVELS * ROWS, dtype=jnp.int32)
    row_open = (cell_index % ROWS < ROWS - 1).astype(jnp.float32)
    level_open = (cell_index // ROWS < LEVELS - 1).astype(jnp.float32)
    row_weight = ROW_DIFFUSION * row_open * sea_float * forward_shift(sea_float, 1)
    level_weight = mixing * level_open * sea_float * forward_shift(sea_float, ROWS)
    return (row_weight, level_weight)


def column_mix(source, row_weight, level_weight):
    row_flux = row_weight * (forward_shift(source, 1) - source)
    level_flux = level_weight * (forward_shift(source, ROWS) - source)
    return row_flux - backward_shift(row_flux, 1) + level_flux - backward_shift(level_flux, ROWS)


def zonal_weights(sea_float, sea_east, velocity):
    opened = sea_float * sea_east
    magnitude = jnp.abs(velocity)
    return jnp.stack(
        [
            opened * (-velocity - magnitude) / 12.0,
            opened * (7.0 * velocity + 3.0 * magnitude) / 12.0,
            opened * (7.0 * velocity - 3.0 * magnitude) / 12.0,
            opened * (magnitude - velocity) / 12.0,
        ]
    )


def trim_rim(source, keep_rim, outer_rim, dimension):
    length = source.shape[dimension] - 2 * outer_rim
    return lax.slice_in_dim(
        source, outer_rim - keep_rim, outer_rim + length + keep_rim, axis=dimension
    )


def surface_slopes(carbon, alkalinity, piston, surface_sea):

    def uptake_of(carbon_in, alkalinity_in):
        return chemistry(carbon_in, alkalinity_in, piston, surface_sea)

    uptake, pullback = jax.vjp(uptake_of, carbon, alkalinity)
    by_carbon, by_alkalinity = pullback(jnp.ones_like(carbon))
    return (uptake, jnp.stack([by_carbon, by_alkalinity]))


def advance_rim(extended, weights, row_weight, level_weight, uptake):
    length = extended.shape[1]
    face_flux = (
        weights[0, 1 : length - 2] * extended[:, 0 : length - 3]
        + weights[1, 1 : length - 2] * extended[:, 1 : length - 2]
        + weights[2, 1 : length - 2] * extended[:, 2 : length - 1]
        + weights[3, 1 : length - 2] * extended[:, 3:length]
    )
    interior = extended[:, 2 : length - 2]
    zonal_term = -(face_flux[:, 1:] - face_flux[:, :-1])
    transported = interior + zonal_term + column_mix(interior, row_weight, level_weight)
    surface_row = transported[0, :, :ROWS] + uptake
    carbon = jnp.concatenate([surface_row, transported[0, :, ROWS:]], axis=-1)
    return jnp.stack([carbon, transported[1]])


def halves(cells, axis, dim, width):
    count = lax.axis_size(axis)
    head = lax.slice_in_dim(cells, 0, width, axis=dim)
    tail = lax.slice_in_dim(cells, cells.shape[dim] - width, cells.shape[dim], axis=dim)
    west = lax.ppermute(tail, axis, [(i, (i + 1) % count) for i in range(count)])
    east = lax.ppermute(head, axis, [((i + 1) % count, i) for i in range(count)])
    return west, east


def lanes_to(source, width):
    pad = [(0, 0)] * source.ndim
    pad[-1] = (0, width - source.shape[-1])
    return jnp.pad(source, pad)


def cell_shift(x, step, lane, forward):
    if forward:
        turned = pltpu.roll(x, 128 - step, 1)
        carried = pltpu.roll(turned, 7, 0)
        return jnp.where(lane >= 128 - step, carried, turned)
    turned = pltpu.roll(x, step, 1)
    carried = pltpu.roll(turned, 1, 0)
    return jnp.where(lane < step, carried, turned)


def retreat_kernel(center_ref, west_ref, east_ref, w_ref, s_ref, seed_ref, out_ref, e_ref, f_ref):
    tracers = center_ref.shape[1]
    local = center_ref.shape[2]
    rim = west_ref.shape[2]
    lane = lax.broadcasted_iota(jnp.int32, (8, 128), 1)

    def step(src, k, stage, o):
        w = [w_ref[m, k] for m in range(8)]
        results = []
        for t in range(tracers):
            x_0 = src[t, k]
            zonal = (
                w[0] * (src[t, k + 2] - src[t, k + 1])
                + w[1] * (src[t, k + 1] - x_0)
                + w[2] * (x_0 - src[t, k - 1])
                + w[3] * (src[t, k - 1] - src[t, k - 2])
            )
            mix = (
                w[4] * (cell_shift(x_0, 1, lane, True) - x_0)
                - w[5] * (x_0 - cell_shift(x_0, 1, lane, False))
                + w[6] * (cell_shift(x_0, ROWS, lane, True) - x_0)
                - w[7] * (x_0 - cell_shift(x_0, ROWS, lane, False))
            )
            forcing = src[0, k] + seed_ref[o, k]
            results.append(x_0 + zonal + mix + s_ref[stage, t, k] * forcing)
        return results

    for o in range(center_ref.shape[0]):
        e_ref[:, rim : rim + local] = center_ref[o]
        e_ref[:, 0:rim] = west_ref[o]
        e_ref[:, rim + local : 2 * rim + local] = east_ref[o]
        for k in range(2, 2 * rim + local - 2):
            for t, value in enumerate(step(e_ref, k, 0, o)):
                f_ref[t, k] = value
        for q in range(0, local, 8):
            rows = [step(f_ref, rim + q + i, 1, o) for i in range(8)]
            for t in range(tracers):
                stacked = jnp.stack([row[t] for row in rows])
                out_ref[o, t, q : q + 8, :] = stacked.reshape(8, stacked.shape[1] * stacked.shape[2])


def two_retreats(center, west, east, stencil, slopes, seeds):
    groups, tracers, local, sub, lanes = center.shape
    rim = west.shape[2]
    span = local + 2 * rim
    pack = 4 if groups % 4 == 0 else 1
    return pl.pallas_call(
        retreat_kernel,
        out_shape=jax.ShapeDtypeStruct((groups, tracers, local, sub * lanes), center.dtype),
        grid=(groups // pack,),
        in_specs=[
            pl.BlockSpec((pack, tracers, local, sub, lanes), lambda g: (g, 0, 0, 0, 0)),
            pl.BlockSpec((pack, tracers, rim, sub, lanes), lambda g: (g, 0, 0, 0, 0)),
            pl.BlockSpec((pack, tracers, rim, sub, lanes), lambda g: (g, 0, 0, 0, 0)),
            pl.BlockSpec(stencil.shape, lambda g: (0, 0, 0, 0)),
            pl.BlockSpec(slopes.shape, lambda g: (0, 0, 0, 0, 0)),
            pl.BlockSpec((pack,) + seeds.shape[1:], lambda g: (g, 0, 0, 0)),
        ],
        out_specs=pl.BlockSpec((pack, tracers, local, sub * lanes), lambda g: (g, 0, 0, 0)),
        scratch_shapes=[
            pltpu.VMEM((tracers, span, sub, lanes), jnp.float32),
            pltpu.VMEM((tracers, span, sub, lanes), jnp.float32),
        ],
    )(center, west, east, stencil, slopes, seeds)


def as_tiles(source):
    return source.reshape(source.shape[:-1] + (source.shape[-1] // 128, 128))


def staged(
    adjoint_in, checkpoint_store, interval, sea_mask, zonal_speed, mixing, piston, cell_area, region
):
    groups = adjoint_in.shape[0]
    cell_count = adjoint_in.shape[3]
    rim_depth = 4
    owners = lax.axis_size("obj")
    owner_index = interval[0] % owners
    band = 2 * ROWS
    stored = lax.dynamic_index_in_dim(checkpoint_store, interval[0] // owners, 0, keepdims=False)
    statics = jnp.concatenate(
        [
            stored[0, :, :band],
            stored[1, :, :band],
            sea_mask.astype(jnp.float32),
            zonal_speed,
            mixing,
            piston,
            cell_area,
            region.astype(jnp.float32),
        ],
        axis=1,
    )
    widened = padded(statics, (("tile", 0),), rim_depth)
    initial_wide = spread(
        jnp.stack([widened[:, :band], widened[:, band : 2 * band]]), "obj", owner_index
    )
    widened = widened[:, 2 * band :]
    sea_wide = widened[:, :cell_count]
    speed_wide = widened[:, cell_count : 2 * cell_count]
    mixing_wide = widened[:, 2 * cell_count : 3 * cell_count]
    offset = 3 * cell_count
    piston_wide = widened[:, offset : offset + ROWS]
    area_wide = widened[:, offset + ROWS : offset + 2 * ROWS]
    region_wide = widened[:, offset + 2 * ROWS : offset + 3 * ROWS]
    sea_east = jnp.concatenate([sea_wide[1:], jnp.zeros_like(sea_wide[:1])], axis=0)
    weights = zonal_weights(sea_wide, sea_east, speed_wide)
    row_weight, level_weight = column_weights(sea_wide, mixing_wide)
    surface_sea = sea_wide[:, :ROWS]
    targets = (lax.axis_index("obj") * groups + jnp.arange(groups, dtype=jnp.int32)).astype(
        jnp.float32
    )
    objective_seeds = area_wide[None] * (region_wide[None] == targets[:, None, None]).astype(
        jnp.float32
    )
    inner_rim = 2
    piston_inner = trim_rim(piston_wide, inner_rim, rim_depth, 0)
    sea_inner = trim_rim(surface_sea, inner_rim, rim_depth, 0)
    initial_inner = trim_rim(initial_wide, inner_rim, rim_depth, 1)
    uptake_first, slopes_first = surface_slopes(
        initial_inner[0, :, :ROWS], initial_inner[1, :, :ROWS], piston_inner, sea_inner
    )
    following = advance_rim(
        initial_wide,
        weights[:, :, :band],
        trim_rim(row_weight, inner_rim, rim_depth, 0)[:, :band],
        trim_rim(level_weight, inner_rim, rim_depth, 0)[:, :band],
        uptake_first,
    )
    _, slopes_second = surface_slopes(
        following[0, :, :ROWS], following[1, :, :ROWS], piston_inner, sea_inner
    )
    west, east = halves(adjoint_in, "tile", 2, rim_depth)
    west, east = as_tiles(west), as_tiles(east)
    span = adjoint_in.shape[2] + 2 * rim_depth

    def along(source, lead):
        pad = [(0, 0)] * source.ndim
        pad[0] = (lead, span - lead - source.shape[0])
        return jnp.pad(source, pad)

    def cells_of(source):
        pad = [(0, 0)] * source.ndim
        pad[-1] = (0, cell_count - source.shape[-1])
        return jnp.pad(source, pad)

    wide = weights.shape[1]
    stencil = as_tiles(
        jnp.stack(
            [
                along(weights[0][1:], 0),
                weights[1],
                along(weights[2][: wide - 1], 1),
                along(weights[3][: wide - 2], 2),
                row_weight,
                backward_shift(row_weight, 1),
                level_weight,
                backward_shift(level_weight, ROWS),
            ]
        )
    )
    second = jnp.moveaxis(slopes_second, 1, 0)
    first_slopes = jnp.moveaxis(trim_rim(slopes_first, 0, inner_rim, 1), 1, 0)
    slopes = as_tiles(
        cells_of(
            jnp.stack(
                [
                    jnp.moveaxis(along(second, inner_rim), 0, 1),
                    jnp.moveaxis(along(first_slopes, rim_depth), 0, 1),
                ]
            )
        )
    )
    seeds = lanes_to(objective_seeds, 128)[:, :, None, :]
    center = as_tiles(adjoint_in)
    return two_retreats(center, west, east, stencil, slopes, seeds)


def solution(mesh):
    placed = (
        P("obj", None, "tile", None),
        P("obj", None, "tile", None),
        P(),
        P("tile", None),
        P("tile", None),
        P("tile", None),
        P("tile", None),
        P("tile", None),
        P("tile", None),
    )
    return jax.shard_map(
        staged, mesh=mesh, in_specs=placed, out_specs=P("obj", None, "tile", None), check_vma=False
    )
```

```python
import jax
import jax.numpy as jnp
from jax import lax
from jax.sharding import PartitionSpec as P
from jax.experimental import pallas as pl
from jax.experimental.pallas import tpu as pltpu

ROWS = 32
LEVELS = 32
NEWTON = 4


DISSOCIATION_ONE = 1400.0
DISSOCIATION_TWO = 1.1
BORATE_CONSTANT = 2.5
BORON_TOTAL = 416.0
AIR_CARBON = 14.0
START_HYDROGEN = 2.0
ROW_DIFFUSION = 0.1


def padded(cells, sides, width):
    for axis, dim in sides:
        count = lax.axis_size(axis)
        head = lax.slice_in_dim(cells, 0, width, axis=dim)
        tail = lax.slice_in_dim(cells, cells.shape[dim] - width, cells.shape[dim], axis=dim)
        cells = jnp.concatenate(
            [
                lax.ppermute(tail, axis, [(i, (i + 1) % count) for i in range(count)]),
                cells,
                lax.ppermute(head, axis, [((i + 1) % count, i) for i in range(count)]),
            ],
            axis=dim,
        )
    return cells


def spread(value, axis, source):
    count = lax.axis_size(axis)
    top = count // 2
    if count < 2 or count & (count - 1):
        kept = jnp.where(lax.axis_index(axis) == source, value, 0).astype(value.dtype)
        return lax.psum(kept, axis)
    rank = jnp.bitwise_xor(lax.axis_index(axis), source)
    moved = lax.ppermute(value, axis, [(i, i ^ top) for i in range(count)])
    value = jnp.where(rank == top, moved, value)
    low = rank & (top - 1)
    received = value
    for mask in range(1, top):
        moved = lax.ppermute(value, axis, [(i, i ^ mask) for i in range(count)])
        received = jnp.where(low == mask, moved, received)
    return received


def chemistry(carbon, alkalinity, piston, surface_sea):
    hydrogen = jnp.full_like(carbon, START_HYDROGEN)
    for _ in range(NEWTON):
        square = hydrogen * hydrogen
        denominator = square + DISSOCIATION_ONE * hydrogen + DISSOCIATION_ONE * DISSOCIATION_TWO
        carbonate = carbon * DISSOCIATION_ONE * (hydrogen + 2.0 * DISSOCIATION_TWO) / denominator
        borate = BORON_TOTAL * BORATE_CONSTANT / (hydrogen + BORATE_CONSTANT)
        derivative = -carbon * DISSOCIATION_ONE * (
            square + 4.0 * DISSOCIATION_TWO * hydrogen + DISSOCIATION_ONE * DISSOCIATION_TWO
        ) / (denominator * denominator) - borate / (hydrogen + BORATE_CONSTANT)
        hydrogen = hydrogen - (carbonate + borate - alkalinity) / derivative
    square = hydrogen * hydrogen
    denominator = square + DISSOCIATION_ONE * hydrogen + DISSOCIATION_ONE * DISSOCIATION_TWO
    dissolved = carbon * square / denominator
    return surface_sea * piston * (AIR_CARBON - dissolved)


def forward_shift(source, offset):
    padding = jnp.zeros(source.shape[:-1] + (offset,), source.dtype)
    return jnp.concatenate([source[..., offset:], padding], axis=-1)


def backward_shift(source, offset):
    padding = jnp.zeros(source.shape[:-1] + (offset,), source.dtype)
    return jnp.concatenate([padding, source[..., :-offset]], axis=-1)


def column_weights(sea_float, mixing):
    cell_index = jnp.arange(LEVELS * ROWS, dtype=jnp.int32)
    row_open = (cell_index % ROWS < ROWS - 1).astype(jnp.float32)
    level_open = (cell_index // ROWS < LEVELS - 1).astype(jnp.float32)
    row_weight = ROW_DIFFUSION * row_open * sea_float * forward_shift(sea_float, 1)
    level_weight = mixing * level_open * sea_float * forward_shift(sea_float, ROWS)
    return (row_weight, level_weight)


def column_mix(source, row_weight, level_weight):
    row_flux = row_weight * (forward_shift(source, 1) - source)
    level_flux = level_weight * (forward_shift(source, ROWS) - source)
    return row_flux - backward_shift(row_flux, 1) + level_flux - backward_shift(level_flux, ROWS)


def zonal_weights(sea_float, sea_east, velocity):
    opened = sea_float * sea_east
    magnitude = jnp.abs(velocity)
    return jnp.stack(
        [
            opened * (-velocity - magnitude) / 12.0,
            opened * (7.0 * velocity + 3.0 * magnitude) / 12.0,
            opened * (7.0 * velocity - 3.0 * magnitude) / 12.0,
            opened * (magnitude - velocity) / 12.0,
        ]
    )


def trim_rim(source, keep_rim, outer_rim, dimension):
    length = source.shape[dimension] - 2 * outer_rim
    return lax.slice_in_dim(
        source, outer_rim - keep_rim, outer_rim + length + keep_rim, axis=dimension
    )


def surface_slopes(carbon, alkalinity, piston, surface_sea):

    def uptake_of(carbon_in, alkalinity_in):
        return chemistry(carbon_in, alkalinity_in, piston, surface_sea)

    uptake, pullback = jax.vjp(uptake_of, carbon, alkalinity)
    by_carbon, by_alkalinity = pullback(jnp.ones_like(carbon))
    return (uptake, jnp.stack([by_carbon, by_alkalinity]))


def advance_rim(extended, weights, row_weight, level_weight, uptake):
    length = extended.shape[1]
    face_flux = (
        weights[0, 1 : length - 2] * extended[:, 0 : length - 3]
        + weights[1, 1 : length - 2] * extended[:, 1 : length - 2]
        + weights[2, 1 : length - 2] * extended[:, 2 : length - 1]
        + weights[3, 1 : length - 2] * extended[:, 3:length]
    )
    interior = extended[:, 2 : length - 2]
    zonal_term = -(face_flux[:, 1:] - face_flux[:, :-1])
    transported = interior + zonal_term + column_mix(interior, row_weight, level_weight)
    surface_row = transported[0, :, :ROWS] + uptake
    carbon = jnp.concatenate([surface_row, transported[0, :, ROWS:]], axis=-1)
    return jnp.stack([carbon, transported[1]])


def halves(cells, axis, dim, width):
    count = lax.axis_size(axis)
    head = lax.slice_in_dim(cells, 0, width, axis=dim)
    tail = lax.slice_in_dim(cells, cells.shape[dim] - width, cells.shape[dim], axis=dim)
    west = lax.ppermute(tail, axis, [(i, (i + 1) % count) for i in range(count)])
    east = lax.ppermute(head, axis, [((i + 1) % count, i) for i in range(count)])
    return west, east


def lanes_to(source, width):
    pad = [(0, 0)] * source.ndim
    pad[-1] = (0, width - source.shape[-1])
    return jnp.pad(source, pad)


def cell_shift(x, step, lane, forward):
    if forward:
        turned = pltpu.roll(x, 128 - step, 1)
        carried = pltpu.roll(turned, 7, 0)
        return jnp.where(lane >= 128 - step, carried, turned)
    turned = pltpu.roll(x, step, 1)
    carried = pltpu.roll(turned, 1, 0)
    return jnp.where(lane < step, carried, turned)


def retreat_kernel(center_ref, west_ref, east_ref, w_ref, s_ref, seed_ref, out_ref, e_ref, f_ref):
    tracers = center_ref.shape[1]
    local = center_ref.shape[2]
    rim = west_ref.shape[2]
    lane = lax.broadcasted_iota(jnp.int32, (8, 128), 1)

    def step(src, k, stage, o):
        w = [w_ref[m, k] for m in range(8)]
        results = []
        for t in range(tracers):
            x_0 = src[t, k]
            zonal = (
                w[0] * (src[t, k + 2] - src[t, k + 1])
                + w[1] * (src[t, k + 1] - x_0)
                + w[2] * (x_0 - src[t, k - 1])
                + w[3] * (src[t, k - 1] - src[t, k - 2])
            )
            mix = (
                w[4] * (cell_shift(x_0, 1, lane, True) - x_0)
                - w[5] * (x_0 - cell_shift(x_0, 1, lane, False))
                + w[6] * (cell_shift(x_0, ROWS, lane, True) - x_0)
                - w[7] * (x_0 - cell_shift(x_0, ROWS, lane, False))
            )
            forcing = src[0, k] + seed_ref[o, k]
            results.append(x_0 + zonal + mix + s_ref[stage, t, k] * forcing)
        return results

    for o in range(center_ref.shape[0]):
        e_ref[:, rim : rim + local] = center_ref[o]
        e_ref[:, 0:rim] = west_ref[o]
        e_ref[:, rim + local : 2 * rim + local] = east_ref[o]
        for k in range(2, 2 * rim + local - 2):
            for t, value in enumerate(step(e_ref, k, 0, o)):
                f_ref[t, k] = value
        for q in range(0, local, 8):
            rows = [step(f_ref, rim + q + i, 1, o) for i in range(8)]
            for t in range(tracers):
                stacked = jnp.stack([row[t] for row in rows])
                out_ref[o, t, q : q + 8, :] = stacked.reshape(8, stacked.shape[1] * stacked.shape[2])


def two_retreats(center, west, east, stencil, slopes, seeds):
    groups, tracers, local, sub, lanes = center.shape
    rim = west.shape[2]
    span = local + 2 * rim
    pack = 4 if groups % 4 == 0 else 1
    return pl.pallas_call(
        retreat_kernel,
        out_shape=jax.ShapeDtypeStruct((groups, tracers, local, sub * lanes), center.dtype),
        grid=(groups // pack,),
        in_specs=[
            pl.BlockSpec((pack, tracers, local, sub, lanes), lambda g: (g, 0, 0, 0, 0)),
            pl.BlockSpec((pack, tracers, rim, sub, lanes), lambda g: (g, 0, 0, 0, 0)),
            pl.BlockSpec((pack, tracers, rim, sub, lanes), lambda g: (g, 0, 0, 0, 0)),
            pl.BlockSpec(stencil.shape, lambda g: (0, 0, 0, 0)),
            pl.BlockSpec(slopes.shape, lambda g: (0, 0, 0, 0, 0)),
            pl.BlockSpec((pack,) + seeds.shape[1:], lambda g: (g, 0, 0, 0)),
        ],
        out_specs=pl.BlockSpec((pack, tracers, local, sub * lanes), lambda g: (g, 0, 0, 0)),
        scratch_shapes=[
            pltpu.VMEM((tracers, span, sub, lanes), jnp.float32),
            pltpu.VMEM((tracers, span, sub, lanes), jnp.float32),
        ],
    )(center, west, east, stencil, slopes, seeds)


def as_tiles(source):
    return source.reshape(source.shape[:-1] + (source.shape[-1] // 128, 128))


def staged(
    adjoint_in, checkpoint_store, interval, sea_mask, zonal_speed, mixing, piston, cell_area, region
):
    groups = adjoint_in.shape[0]
    cell_count = adjoint_in.shape[3]
    rim_depth = 4
    owners = lax.axis_size("obj")
    owner_index = interval[0] % owners
    band = 2 * ROWS
    stored = lax.dynamic_index_in_dim(checkpoint_store, interval[0] // owners, 0, keepdims=False)
    whole = jnp.concatenate([sea_mask, region], axis=1).astype(jnp.float32)
    statics = jnp.concatenate(
        [
            stored[0, :, :band],
            stored[1, :, :band],
            whole[:, :cell_count],
            zonal_speed,
            mixing,
            piston,
            cell_area,
            whole[:, cell_count:],
        ],
        axis=1,
    )
    widened = padded(statics, (("tile", 0),), rim_depth)
    initial_wide = spread(
        jnp.stack([widened[:, :band], widened[:, band : 2 * band]]), "obj", owner_index
    )
    widened = widened[:, 2 * band :]
    sea_wide = widened[:, :cell_count]
    speed_wide = widened[:, cell_count : 2 * cell_count]
    mixing_wide = widened[:, 2 * cell_count : 3 * cell_count]
    offset = 3 * cell_count
    piston_wide = widened[:, offset : offset + ROWS]
    area_wide = widened[:, offset + ROWS : offset + 2 * ROWS]
    region_wide = widened[:, offset + 2 * ROWS : offset + 3 * ROWS]
    sea_east = jnp.concatenate([sea_wide[1:], jnp.zeros_like(sea_wide[:1])], axis=0)
    weights = zonal_weights(sea_wide, sea_east, speed_wide)
    row_weight, level_weight = column_weights(sea_wide, mixing_wide)
    surface_sea = sea_wide[:, :ROWS]
    targets = (lax.axis_index("obj") * groups + jnp.arange(groups, dtype=jnp.int32)).astype(
        jnp.float32
    )
    objective_seeds = area_wide[None] * (region_wide[None] == targets[:, None, None]).astype(
        jnp.float32
    )
    inner_rim = 2
    piston_inner = trim_rim(piston_wide, inner_rim, rim_depth, 0)
    sea_inner = trim_rim(surface_sea, inner_rim, rim_depth, 0)
    initial_inner = trim_rim(initial_wide, inner_rim, rim_depth, 1)
    uptake_first, slopes_first = surface_slopes(
        initial_inner[0, :, :ROWS], initial_inner[1, :, :ROWS], piston_inner, sea_inner
    )
    following = advance_rim(
        initial_wide,
        weights[:, :, :band],
        trim_rim(row_weight, inner_rim, rim_depth, 0)[:, :band],
        trim_rim(level_weight, inner_rim, rim_depth, 0)[:, :band],
        uptake_first,
    )
    _, slopes_second = surface_slopes(
        following[0, :, :ROWS], following[1, :, :ROWS], piston_inner, sea_inner
    )
    west, east = halves(as_tiles(adjoint_in), "tile", 2, rim_depth)
    span = adjoint_in.shape[2] + 2 * rim_depth

    def along(source, lead):
        pad = [(0, 0)] * source.ndim
        pad[0] = (lead, span - lead - source.shape[0])
        return jnp.pad(source, pad)

    def cells_of(source):
        pad = [(0, 0)] * source.ndim
        pad[-1] = (0, cell_count - source.shape[-1])
        return jnp.pad(source, pad)

    wide = weights.shape[1]
    stencil = as_tiles(
        jnp.stack(
            [
                along(weights[0][1:], 0),
                weights[1],
                along(weights[2][: wide - 1], 1),
                along(weights[3][: wide - 2], 2),
                row_weight,
                backward_shift(row_weight, 1),
                level_weight,
                backward_shift(level_weight, ROWS),
            ]
        )
    )
    second = jnp.moveaxis(slopes_second, 1, 0)
    first_slopes = jnp.moveaxis(trim_rim(slopes_first, 0, inner_rim, 1), 1, 0)
    slopes = as_tiles(
        cells_of(
            jnp.stack(
                [
                    jnp.moveaxis(along(second, inner_rim), 0, 1),
                    jnp.moveaxis(along(first_slopes, rim_depth), 0, 1),
                ]
            )
        )
    )
    seeds = lanes_to(objective_seeds, 128)[:, :, None, :]
    return two_retreats(as_tiles(adjoint_in), west, east, stencil, slopes, seeds)


def solution(mesh):
    placed = (
        P("obj", None, "tile", None),
        P("obj", None, "tile", None),
        P(),
        P("tile", None),
        P("tile", None),
        P("tile", None),
        P("tile", None),
        P("tile", None),
        P("tile", None),
    )
    return jax.shard_map(
        staged, mesh=mesh, in_specs=placed, out_specs=P("obj", None, "tile", None), check_vma=False
    )
```
